128 devices in a mesh: rows: 8 (over x, z_hi), cols: 8 (over y, core), rep: 2 (over z_lo).
Axes of the slice: x: 4, y: 4, z: 4 (z_hi: 2, z_lo: 2; z = z_hi * 2 + z_lo), core: 2. Of those that a mesh axis runs over, the one named last changes fastest.
Arguments:
- inputs: bfloat16 [8, 128, 256, 256], P('rep', 'rows', 'cols'), may hold values from -6 to 6
- upstream: bfloat16 [8, 128, 256, 256], P('rep', 'rows', 'cols'), may hold values from -6 to 6
- kernel: bfloat16 [3, 3, 256, 256], replicated, may hold values from -0.125 to 0.125
- probe_init: float32 [128, 256, 256], P('rows', 'cols'), may hold values from -18 to 18
Outputs:
- outputs: bfloat16 [8, 128, 256, 256], P('rep', 'rows', 'cols')
- input_grad: bfloat16 [8, 128, 256, 256], P('rep', 'rows', 'cols')
- kernel_grad: float32 [256, 2304], P(('rows', 'cols'))
- probe_out: float32 [128, 256, 256], P('rows', 'cols')
- lipschitz: float32 [], replicated
- norm_trace: float32 [3], replicated
The draws below stay inside these ranges and needn't reach their ends.
All inputs are finite; a program needn't handle non-finite values.
Results may differ from the reference program's by a relative error of at most 0.011.
Values may be sent and summed in bfloat16 or wider, within the bound.
No kernel may reach another device: no remote copies, remote signals or barrier semaphores. Data moves between devices by JAX's collectives and lax.ppermute only.
A program may use at most 128 MiB of HBM per device.

```python
import jax
import jax.numpy as jnp

C = 256
ITERS = 4
NH = 128
NW = 256
BATCH = 8


def draw_probe_init(key, part):
    ramp = jnp.arange(NH, dtype=jnp.float32) / max(NH - 1, 1)
    row_scale = 1.0 + 2.0 * ramp
    sample = jax.random.normal(key, (NH, NW, C), jnp.float32)
    return jnp.clip(sample * row_scale[:, None, None], -18.0, 18.0)


def raised(result, key, source, target, shards_of, factor):
    owner, partner = [(jnp.arange(result.shape[dim]) // (result.shape[dim] // shards_of)).reshape([-1 if axis == dim else 1 for axis in range(result.ndim)]) for dim in (source, target)]
    chosen = jax.random.permutation(key, shards_of)[partner]
    strong = (owner == chosen) | (owner == (partner + shards_of // 2) % shards_of)
    return jnp.where(strong, factor * result, result)


def block_levels(rng, shape, split, least, largest):
    gain = 1.0
    for dim, parts in split:
        heights = jax.random.uniform(jax.random.fold_in(jax.random.fold_in(rng, 6), dim), (parts,), jnp.float32, least / len(split), largest / len(split))
        gain = gain * jnp.repeat(jnp.exp(heights), shape[dim] // parts).reshape((-1,) + (1,) * (len(shape) - 1 - dim))
    return gain


def scatter_about(own_key, extent, deviation, reach, cuts=(), held_as=jnp.bfloat16):
    entries = jax.random.normal(own_key, extent, jnp.float32) * deviation
    if len(cuts) > 0:
        entries = block_levels(own_key, extent, cuts, -0.22, 0.18) * entries
    return jnp.clip(entries, min=-reach, max=reach).astype(held_as)


def gaussian_with(key, shape, scale, most, shards, heavy, held_as=jnp.bfloat16):
    result = scale * jax.random.normal(key, shape, jnp.float32)
    if shards:
        result = result * block_levels(key, shape, shards, -0.22, 0.18)
    return jnp.clip(raised(result, jax.random.fold_in(key, 3), *heavy), -most, most).astype(held_as)


def setup_inputs(seed: int = 0) -> dict:
    arg_keys = jax.random.split(jax.random.key(seed), 5)
    return {
        "inputs": scatter_about(arg_keys[0], (BATCH, NH, NW, C), 1.0, 6.0, ((0, 2), (1, 8), (2, 8))),
        "upstream": gaussian_with(arg_keys[1], (BATCH, NH, NW, C), 1.0, 6.0, ((0, 2), (1, 8), (2, 8)), (1, 3, 8, 2.0)),
        "kernel": scatter_about(arg_keys[2], (3, 3, C, C), (9 * C) ** -0.5, 0.125),
        "probe_init": draw_probe_init(jax.random.fold_in(arg_keys[4], 71), 0),
    }


def spatial_pad(field, periodic):
    widths = [(0, 0)] * (field.ndim - 3) + [(1, 1), (1, 1), (0, 0)]
    if periodic:
        return jnp.pad(field, widths, mode='wrap')
    return jnp.pad(field, widths)

def tap_sum(padded, kernel, height, breadth, adjoint):
    summed = None
    for row_tap in range(3):
        for col_tap in range(3):
            weights = kernel[row_tap, col_tap].astype(jnp.float32)
            if adjoint:
                window = padded[..., 2 - row_tap:2 - row_tap + height, 2 - col_tap:2 - col_tap + breadth, :]
                contrib = jnp.einsum('...d,cd->...c', window.astype(jnp.float32), weights)
            else:
                window = padded[..., row_tap:row_tap + height, col_tap:col_tap + breadth, :]
                contrib = jnp.einsum('...c,cd->...d', window.astype(jnp.float32), weights)
            summed = contrib if summed is None else summed + contrib
    return summed

def reference(inputs, upstream, kernel, probe_init):
    count = NH * NW * C
    iterate = probe_init.astype(jnp.bfloat16)
    back = None
    traces = []
    for iteration in range(ITERS):
        image = tap_sum(spatial_pad(iterate, True), kernel, NH, NW, False).astype(jnp.bfloat16)
        back = tap_sum(spatial_pad(image, True), kernel, NH, NW, True)
        if iteration + 1 < ITERS:
            scale_now = jnp.sqrt(jnp.sum(back * back) / count + 1e-06)
            traces.append(scale_now)
            iterate = (back / scale_now).astype(jnp.bfloat16)
    norm_trace = jnp.stack(traces).astype(jnp.float32)
    sum_back = jnp.sum(back * back)
    wide_iter = iterate.astype(jnp.float32)
    sum_probe = jnp.sum(wide_iter * wide_iter)
    lipschitz = jnp.sqrt(jnp.sqrt(sum_back / sum_probe))
    probe_out = back / jnp.sqrt(sum_back / count + 1e-06)
    padded_in = spatial_pad(inputs, False)
    outputs = tap_sum(padded_in, kernel, NH, NW, False).astype(jnp.bfloat16)
    input_grad = tap_sum(spatial_pad(upstream, False), kernel, NH, NW, True).astype(jnp.bfloat16)
    wide_up = upstream.astype(jnp.float32)
    pieces = []
    for row_tap in range(3):
        for col_tap in range(3):
            window = padded_in[:, row_tap:row_tap + NH, col_tap:col_tap + NW, :].astype(jnp.float32)
            pieces.append(jnp.einsum('nhwd,nhwc->dc', wide_up, window))
    stacked = jnp.stack(pieces, axis=1).reshape(C, 9 * C)
    kernel_grad = stacked * (1.0 / jnp.sqrt(jnp.float32(BATCH * NH * NW)))
    return (outputs, input_grad, kernel_grad, probe_out, lipschitz, norm_trace)
```

```python
import math

import jax
import jax.numpy as jnp
from jax import lax
from jax.sharding import PartitionSpec as P

ITERS = 4


def extended(cells, sides, width, closed):
    for axis, dim in sides:
        count = lax.axis_size(axis)
        ends = count if closed else count - 1
        head = lax.slice_in_dim(cells, 0, width, axis=dim)
        tail = lax.slice_in_dim(cells, cells.shape[dim] - width, cells.shape[dim], axis=dim)
        cells = jnp.concatenate(
            [
                lax.ppermute(tail, axis, [(i, (i + 1) % count) for i in range(ends)]),
                cells,
                lax.ppermute(head, axis, [((i + 1) % count, i) for i in range(ends)]),
            ],
            axis=dim,
        )
    return cells


def butterfly_sum(value, axes):
    for axis in axes:
        count = lax.axis_size(axis)
        step = 1
        while step < count:
            value = value + lax.ppermute(value, axis, [(i, i ^ step) for i in range(count)])
            step *= 2
    return value


def halving_scatter(value, axes):
    for axis in axes:
        count = lax.axis_size(axis)
        index = lax.axis_index(axis)
        step = count // 2
        while step >= 1:
            half = value.shape[0] // 2
            upper = (index // step) % 2
            keep = lax.dynamic_slice_in_dim(value, upper * half, half, axis=0)
            send = lax.dynamic_slice_in_dim(value, (1 - upper) * half, half, axis=0)
            value = keep + lax.ppermute(send, axis, [(i, i ^ step) for i in range(count)])
            step //= 2
    return value


def tap_sum(padded, kernel, height, breadth, adjoint):
    summed = None
    for row_tap in range(3):
        for col_tap in range(3):
            if adjoint:
                window = padded[
                    ..., 2 - row_tap : 2 - row_tap + height, 2 - col_tap : 2 - col_tap + breadth, :
                ]
                contrib = jnp.einsum(
                    "...d,cd->...c",
                    window,
                    kernel[row_tap, col_tap],
                    preferred_element_type=jnp.float32,
                )
            else:
                window = padded[..., row_tap : row_tap + height, col_tap : col_tap + breadth, :]
                contrib = jnp.einsum(
                    "...c,cd->...d",
                    window,
                    kernel[row_tap, col_tap],
                    preferred_element_type=jnp.float32,
                )
            summed = contrib if summed is None else summed + contrib
    return summed


def per_device(inputs, upstream, kernel, probe_init):
    height = inputs.shape[1]
    breadth = inputs.shape[2]
    channels = kernel.shape[2]
    rows_count = lax.axis_size("rows")
    cols_count = lax.axis_size("cols")
    count = float(height * rows_count * breadth * cols_count * channels)
    iterate = probe_init.astype(jnp.bfloat16)
    back = None
    traces = []
    local_sums = []
    for iteration in range(ITERS):
        padded_probe = extended(iterate, (("rows", 0), ("cols", 1)), 1, True)
        image = tap_sum(padded_probe, kernel, height, breadth, False).astype(jnp.bfloat16)
        padded_image = extended(image, (("rows", 0), ("cols", 1)), 1, True)
        back = tap_sum(padded_image, kernel, height, breadth, True)
        if iteration + 1 < ITERS:
            squared = butterfly_sum(jnp.sum(back * back), ("rows", "cols"))
            scale_now = jnp.sqrt(squared / count + 1e-06)
            traces.append(scale_now)
            iterate = (back / scale_now).astype(jnp.bfloat16)
    wide_iter = iterate.astype(jnp.float32)
    totals = butterfly_sum(
        jnp.stack([jnp.sum(back * back), jnp.sum(wide_iter * wide_iter)] + local_sums),
        ("rows", "cols"),
    )
    sum_back = totals[0]
    sum_probe = totals[1]
    norm_trace = jnp.stack(traces)
    lipschitz = jnp.sqrt(jnp.sqrt(sum_back / sum_probe))
    probe_out = back / jnp.sqrt(sum_back / count + 1e-06)
    padded_in = extended(inputs, (("rows", 1), ("cols", 2)), 1, False)
    outputs = tap_sum(padded_in, kernel, height, breadth, False).astype(jnp.bfloat16)
    padded_up = extended(upstream, (("rows", 1), ("cols", 2)), 1, False)
    input_grad = tap_sum(padded_up, kernel, height, breadth, True).astype(jnp.bfloat16)
    pieces = []
    for row_tap in range(3):
        for col_tap in range(3):
            window = padded_in[:, row_tap : row_tap + height, col_tap : col_tap + breadth, :]
            pieces.append(
                jnp.einsum("nhwd,nhwc->dc", upstream, window, preferred_element_type=jnp.float32)
            )
    local_grad = jnp.stack(pieces, axis=1).reshape(channels, 9 * channels)
    owned = halving_scatter(local_grad, ("rows", "cols"))
    owned = butterfly_sum(owned, ("rep",))
    total_cells = (
        inputs.shape[0] * lax.axis_size("rep") * height * rows_count * breadth * cols_count
    )
    kernel_grad = owned * (1.0 / math.sqrt(total_cells))
    return (outputs, input_grad, kernel_grad, probe_out, lipschitz, norm_trace)


def solution(mesh):
    placed = (
        P("rep", "rows", "cols", None),
        P("rep", "rows", "cols", None),
        P(),
        P("rows", "cols", None),
    )
    return jax.shard_map(
        per_device,
        mesh=mesh,
        in_specs=placed,
        out_specs=(
            P("rep", "rows", "cols", None),
            P("rep", "rows", "cols", None),
            P(("rows", "cols"), None),
            P("rows", "cols", None),
            P(),
            P(),
        ),
        check_vma=False,
    )
```

```python
import math

import jax
import jax.numpy as jnp
from jax import lax
from jax.sharding import PartitionSpec as P

ITERS = 4


def extended(cells, sides, width, closed):
    for axis, dim in sides:
        count = lax.axis_size(axis)
        ends = count if closed else count - 1
        head = lax.slice_in_dim(cells, 0, width, axis=dim)
        tail = lax.slice_in_dim(cells, cells.shape[dim] - width, cells.shape[dim], axis=dim)
        cells = jnp.concatenate(
            [
                lax.ppermute(tail, axis, [(i, (i + 1) % count) for i in range(ends)]),
                cells,
                lax.ppermute(head, axis, [((i + 1) % count, i) for i in range(ends)]),
            ],
            axis=dim,
        )
    return cells


def butterfly_sum(value, axes):
    for axis in axes:
        count = lax.axis_size(axis)
        step = 1
        while step < count:
            value = value + lax.ppermute(value, axis, [(i, i ^ step) for i in range(count)])
            step *= 2
    return value


def halving_scatter(value, axes):
    for axis in axes:
        count = lax.axis_size(axis)
        index = lax.axis_index(axis)
        step = count // 2
        while step >= 1:
            half = value.shape[0] // 2
            upper = (index // step) % 2
            keep = lax.dynamic_slice_in_dim(value, upper * half, half, axis=0)
            send = lax.dynamic_slice_in_dim(value, (1 - upper) * half, half, axis=0)
            value = keep + lax.ppermute(send, axis, [(i, i ^ step) for i in range(count)])
            step //= 2
    return value


def tap_sum(padded, kernel, height, breadth, adjoint):
    summed = None
    for row_tap in range(3):
        for col_tap in range(3):
            if adjoint:
                window = padded[
                    ..., 2 - row_tap : 2 - row_tap + height, 2 - col_tap : 2 - col_tap + breadth, :
                ]
                contrib = jnp.einsum(
                    "...d,cd->...c",
                    window,
                    kernel[row_tap, col_tap],
                    preferred_element_type=jnp.float32,
                )
            else:
                window = padded[..., row_tap : row_tap + height, col_tap : col_tap + breadth, :]
                contrib = jnp.einsum(
                    "...c,cd->...d",
                    window,
                    kernel[row_tap, col_tap],
                    preferred_element_type=jnp.float32,
                )
            summed = contrib if summed is None else summed + contrib
    return summed


def per_device(inputs, upstream, kernel, probe_init):
    height = inputs.shape[1]
    breadth = inputs.shape[2]
    channels = kernel.shape[2]
    rows_count = lax.axis_size("rows")
    cols_count = lax.axis_size("cols")
    count = float(height * rows_count * breadth * cols_count * channels)
    field = (("rows", 0), ("cols", 1))
    iterate = probe_init.astype(jnp.bfloat16)
    padded_probe = extended(iterate, field, 2, True)
    back = None
    traces = []
    local_sums = []
    for iteration in range(ITERS):
        image = tap_sum(padded_probe, kernel, height + 2, breadth + 2, False).astype(jnp.bfloat16)
        back = tap_sum(image, kernel, height, breadth, True)
        if iteration + 1 < ITERS:
            padded_back = extended(back, field, 2, True)
            squared = butterfly_sum(jnp.sum(back * back), ("rows", "cols"))
            scale_now = jnp.sqrt(squared / count + 1e-06)
            traces.append(scale_now)
            iterate = (back / scale_now).astype(jnp.bfloat16)
            padded_probe = (padded_back / scale_now).astype(jnp.bfloat16)
    wide_iter = iterate.astype(jnp.float32)
    totals = butterfly_sum(
        jnp.stack([jnp.sum(back * back), jnp.sum(wide_iter * wide_iter)] + local_sums),
        ("rows", "cols"),
    )
    sum_back = totals[0]
    sum_probe = totals[1]
    norm_trace = jnp.stack(traces)
    lipschitz = jnp.sqrt(jnp.sqrt(sum_back / sum_probe))
    probe_out = back / jnp.sqrt(sum_back / count + 1e-06)
    padded_in = extended(inputs, (("rows", 1), ("cols", 2)), 1, False)
    outputs = tap_sum(padded_in, kernel, height, breadth, False).astype(jnp.bfloat16)
    padded_up = extended(upstream, (("rows", 1), ("cols", 2)), 1, False)
    input_grad = tap_sum(padded_up, kernel, height, breadth, True).astype(jnp.bfloat16)
    pieces = []
    for row_tap in range(3):
        for col_tap in range(3):
            window = padded_in[:, row_tap : row_tap + height, col_tap : col_tap + breadth, :]
            pieces.append(
                jnp.einsum("nhwd,nhwc->dc", upstream, window, preferred_element_type=jnp.float32)
            )
    local_grad = jnp.stack(pieces, axis=1).reshape(channels, 9 * channels)
    owned = lax.psum_scatter(local_grad, "rows", scatter_dimension=0, tiled=True)
    owned = lax.psum_scatter(owned, "cols", scatter_dimension=0, tiled=True)
    owned = butterfly_sum(owned, ("rep",))
    total_cells = (
        inputs.shape[0] * lax.axis_size("rep") * height * rows_count * breadth * cols_count
    )
    kernel_grad = owned * (1.0 / math.sqrt(total_cells))
    return (outputs, input_grad, kernel_grad, probe_out, lipschitz, norm_trace)


def solution(mesh):
    placed = (
        P("rep", "rows", "cols", None),
        P("rep", "rows", "cols", None),
        P(),
        P("rows", "cols", None),
    )
    return jax.shard_map(
        per_device,
        mesh=mesh,
        in_specs=placed,
        out_specs=(
            P("rep", "rows", "cols", None),
            P("rep", "rows", "cols", None),
            P(("rows", "cols"), None),
            P("rows", "cols", None),
            P(),
            P(),
        ),
        check_vma=False,
    )
```

```python
import math

import jax
import jax.numpy as jnp
from jax import lax
from jax.sharding import PartitionSpec as P

ITERS = 4


def extended(cells, sides, width, closed):
    for axis, dim in sides:
        count = lax.axis_size(axis)
        ends = count if closed else count - 1
        head = lax.slice_in_dim(cells, 0, width, axis=dim)
        tail = lax.slice_in_dim(cells, cells.shape[dim] - width, cells.shape[dim], axis=dim)
        cells = jnp.concatenate(
            [
                lax.ppermute(tail, axis, [(i, (i + 1) % count) for i in range(ends)]),
                cells,
                lax.ppermute(head, axis, [((i + 1) % count, i) for i in range(ends)]),
            ],
            axis=dim,
        )
    return cells


def butterfly_sum(value, axes):
    for axis in axes:
        count = lax.axis_size(axis)
        step = 1
        while step < count:
            value = value + lax.ppermute(value, axis, [(i, i ^ step) for i in range(count)])
            step *= 2
    return value


def halving_scatter(value, axes):
    for axis in axes:
        count = lax.axis_size(axis)
        index = lax.axis_index(axis)
        step = count // 2
        while step >= 1:
            half = value.shape[0] // 2
            upper = (index // step) % 2
            keep = lax.dynamic_slice_in_dim(value, upper * half, half, axis=0)
            send = lax.dynamic_slice_in_dim(value, (1 - upper) * half, half, axis=0)
            value = keep + lax.ppermute(send, axis, [(i, i ^ step) for i in range(count)])
            step //= 2
    return value


def conv(padded, weights, adjoint):
    if adjoint:
        weights = weights[::-1, ::-1]
    return lax.conv_general_dilated(
        padded,
        weights,
        window_strides=(1, 1),
        padding="VALID",
        dimension_numbers=("NHWC", "HWOI" if adjoint else "HWIO", "NHWC"),
        preferred_element_type=jnp.float32,
    )


def per_device(inputs, upstream, kernel, probe_init):
    batch = inputs.shape[0]
    height = inputs.shape[1]
    breadth = inputs.shape[2]
    channels = kernel.shape[2]
    rows_count = lax.axis_size("rows")
    cols_count = lax.axis_size("cols")
    count = float(height * rows_count * breadth * cols_count * channels)
    field = (("rows", 0), ("cols", 1))
    iterate = probe_init.astype(jnp.bfloat16)
    padded_probe = extended(iterate, field, 2, True)
    back = None
    traces = []
    for iteration in range(ITERS):
        image = conv(padded_probe[None], kernel, False).astype(jnp.bfloat16)
        back = conv(image, kernel, True)[0]
        if iteration + 1 < ITERS:
            padded_back = extended(back, field, 2, True)
            squared = butterfly_sum(jnp.sum(back * back), ("rows", "cols"))
            scale_now = jnp.sqrt(squared / count + 1e-06)
            traces.append(scale_now)
            iterate = (back / scale_now).astype(jnp.bfloat16)
            padded_probe = (padded_back / scale_now).astype(jnp.bfloat16)
    wide_iter = iterate.astype(jnp.float32)
    totals = butterfly_sum(
        jnp.stack([jnp.sum(back * back), jnp.sum(wide_iter * wide_iter)]),
        ("rows", "cols"),
    )
    sum_back = totals[0]
    sum_probe = totals[1]
    norm_trace = jnp.stack(traces)
    lipschitz = jnp.sqrt(jnp.sqrt(sum_back / sum_probe))
    probe_out = back / jnp.sqrt(sum_back / count + 1e-06)
    padded_both = extended(
        jnp.concatenate([inputs, upstream], axis=0), (("rows", 1), ("cols", 2)), 1, False
    )
    padded_in = padded_both[:batch]
    padded_up = padded_both[batch:]
    outputs = conv(padded_in, kernel, False).astype(jnp.bfloat16)
    input_grad = conv(padded_up, kernel, True).astype(jnp.bfloat16)
    local_grad = lax.conv_general_dilated(
        padded_in,
        upstream,
        window_strides=(1, 1),
        padding="VALID",
        dimension_numbers=("CHWN", "IHWO", "CHWN"),
        preferred_element_type=jnp.float32,
    ).reshape(channels, 9 * channels)
    owned = halving_scatter(local_grad, ("rows", "cols"))
    owned = butterfly_sum(owned, ("rep",))
    total_cells = batch * lax.axis_size("rep") * height * rows_count * breadth * cols_count
    kernel_grad = owned * (1.0 / math.sqrt(total_cells))
    return (outputs, input_grad, kernel_grad, probe_out, lipschitz, norm_trace)


def solution(mesh):
    placed = (
        P("rep", "rows", "cols", None),
        P("rep", "rows", "cols", None),
        P(),
        P("rows", "cols", None),
    )
    return jax.shard_map(
        per_device,
        mesh=mesh,
        in_specs=placed,
        out_specs=(
            P("rep", "rows", "cols", None),
            P("rep", "rows", "cols", None),
            P(("rows", "cols"), None),
            P("rows", "cols", None),
            P(),
            P(),
        ),
        check_vma=False,
    )
```

```python
import math

import jax
import jax.numpy as jnp
from jax import lax
from jax.sharding import PartitionSpec as P

ITERS = 4


def extended(cells, sides, width, closed):
    for axis, dim in sides:
        count = lax.axis_size(axis)
        ends = count if closed else count - 1
        head = lax.slice_in_dim(cells, 0, width, axis=dim)
        tail = lax.slice_in_dim(cells, cells.shape[dim] - width, cells.shape[dim], axis=dim)
        cells = jnp.concatenate(
            [
                lax.ppermute(tail, axis, [(i, (i + 1) % count) for i in range(ends)]),
                cells,
                lax.ppermute(head, axis, [((i + 1) % count, i) for i in range(ends)]),
            ],
            axis=dim,
        )
    return cells


def butterfly_sum(value, axes, tasks=None):
    for axis in axes:
        count = lax.axis_size(axis)
        step = 1
        while step < count:
            pairs = [(i, i ^ step) for i in range(count)]
            if tasks:
                args, work, sink = tasks.pop(0)()
                value, args = lax.optimization_barrier((value, args))
                received = lax.ppermute(value, axis, pairs)
                received, result = lax.optimization_barrier((received, work(*args)))
                sink(result)
            else:
                received = lax.ppermute(value, axis, pairs)
            value = value + received
            step *= 2
    return value


def halving_step(value, axis, step):
    count = lax.axis_size(axis)
    index = lax.axis_index(axis)
    half = value.shape[0] // 2
    upper = (index // step) % 2
    keep = lax.dynamic_slice_in_dim(value, upper * half, half, axis=0)
    send = lax.dynamic_slice_in_dim(value, (1 - upper) * half, half, axis=0)
    return keep + lax.ppermute(send, axis, [(i, i ^ step) for i in range(count)])


def conv(padded, weights, adjoint):
    if adjoint:
        weights = weights[::-1, ::-1]
    return lax.conv_general_dilated(
        padded,
        weights,
        window_strides=(1, 1),
        padding="VALID",
        dimension_numbers=("NHWC", "HWOI" if adjoint else "HWIO", "NHWC"),
        preferred_element_type=jnp.float32,
    )


def weight_conv(padded_in, up):
    channels = up.shape[-1]
    return lax.conv_general_dilated(
        padded_in,
        up,
        window_strides=(1, 1),
        padding="VALID",
        dimension_numbers=("CHWN", "IHWO", "CHWN"),
        preferred_element_type=jnp.float32,
    ).reshape(channels, 9 * padded_in.shape[-1])


def per_device(inputs, upstream, kernel, probe_init):
    batch = inputs.shape[0]
    height = inputs.shape[1]
    breadth = inputs.shape[2]
    rows_count = lax.axis_size("rows")
    cols_count = lax.axis_size("cols")
    count = float(height * rows_count * breadth * cols_count * kernel.shape[2])
    state = {"both": jnp.concatenate([inputs, upstream], axis=0), "out": {}, "grad": {}}
    tasks = []

    def put(store, key):
        def sink(result):
            store[key] = result

        return sink

    def halo_task(side):
        def make():
            def work(cells):
                return extended(cells, (side,), 1, False)

            return (state["both"],), work, put(state, "both")

        return make

    tasks.append(halo_task(("rows", 1)))
    tasks.append(halo_task(("cols", 2)))

    def conv_task(kind, snap):
        def make():
            first = snap if kind == "out" else batch + snap

            def work(cells):
                return conv(cells, kernel, kind == "grad").astype(jnp.bfloat16)

            return (state["both"][first : first + 1],), work, put(state[kind], snap)

        return make

    for snap in range(batch):
        tasks.append(conv_task("out", snap))
    for snap in range(batch):
        tasks.append(conv_task("grad", snap))

    middle = batch // 2

    def weight_task(first, last):
        def make():
            args = (state["both"][first:last], upstream[first:last])
            return args, weight_conv, put(state, ("w", first))

        return make

    tasks.append(weight_task(0, middle))
    tasks.append(weight_task(middle, batch))

    def halving_task(axis, step):
        def make():
            if "kgrad" in state:
                value = state["kgrad"]
            else:
                value = state[("w", 0)] + state[("w", middle)]

            def work(value):
                return halving_step(value, axis, step)

            return (value,), work, put(state, "kgrad")

        return make

    for axis in ("rows", "cols"):
        step = lax.axis_size(axis) // 2
        while step >= 1:
            tasks.append(halving_task(axis, step))
            step //= 2

    def rep_task():
        def work(value):
            return butterfly_sum(value, ("rep",))

        return (state["kgrad"],), work, put(state, "kgrad")

    tasks.append(rep_task)

    field = (("rows", 0), ("cols", 1))
    iterate = probe_init.astype(jnp.bfloat16)
    padded_probe = extended(iterate, field, 2, True)
    back = None
    traces = []
    for iteration in range(ITERS):
        image = conv(padded_probe[None], kernel, False).astype(jnp.bfloat16)
        back = conv(image, kernel, True)[0]
        if iteration + 1 < ITERS:
            padded_back = extended(back, field, 2, True)
            squared = butterfly_sum(jnp.sum(back * back), ("rows", "cols"), tasks)
            scale_now = jnp.sqrt(squared / count + 1e-06)
            traces.append(scale_now)
            iterate = (back / scale_now).astype(jnp.bfloat16)
            padded_probe = (padded_back / scale_now).astype(jnp.bfloat16)
    wide_iter = iterate.astype(jnp.float32)
    totals = butterfly_sum(
        jnp.stack([jnp.sum(back * back), jnp.sum(wide_iter * wide_iter)]),
        ("rows", "cols"),
        tasks,
    )
    while tasks:
        args, work, sink = tasks.pop(0)()
        sink(work(*args))
    sum_back = totals[0]
    sum_probe = totals[1]
    norm_trace = jnp.stack(traces)
    lipschitz = jnp.sqrt(jnp.sqrt(sum_back / sum_probe))
    probe_out = back / jnp.sqrt(sum_back / count + 1e-06)
    outputs = jnp.concatenate([state["out"][snap] for snap in range(batch)], axis=0)
    input_grad = jnp.concatenate([state["grad"][snap] for snap in range(batch)], axis=0)
    total_cells = batch * lax.axis_size("rep") * height * rows_count * breadth * cols_count
    kernel_grad = state["kgrad"] * (1.0 / math.sqrt(total_cells))
    return (outputs, input_grad, kernel_grad, probe_out, lipschitz, norm_trace)


def solution(mesh):
    placed = (
        P("rep", "rows", "cols", None),
        P("rep", "rows", "cols", None),
        P(),
        P("rows", "cols", None),
    )
    return jax.shard_map(
        per_device,
        mesh=mesh,
        in_specs=placed,
        out_specs=(
            P("rep", "rows", "cols", None),
            P("rep", "rows", "cols", None),
            P(("rows", "cols"), None),
            P("rows", "cols", None),
            P(),
            P(),
        ),
        check_vma=False,
    )
```

```python
import math

import jax
import jax.numpy as jnp
from jax import lax
from jax.sharding import PartitionSpec as P

ITERS = 4


def extended(cells, sides, width, closed):
    for axis, dim in sides:
        count = lax.axis_size(axis)
        ends = count if closed else count - 1
        head = lax.slice_in_dim(cells, 0, width, axis=dim)
        tail = lax.slice_in_dim(cells, cells.shape[dim] - width, cells.shape[dim], axis=dim)
        cells = jnp.concatenate(
            [
                lax.ppermute(tail, axis, [(i, (i + 1) % count) for i in range(ends)]),
                cells,
                lax.ppermute(head, axis, [((i + 1) % count, i) for i in range(ends)]),
            ],
            axis=dim,
        )
    return cells


def butterfly_sum(value, axes):
    for axis in axes:
        count = lax.axis_size(axis)
        step = 1
        while step < count:
            value = value + lax.ppermute(value, axis, [(i, i ^ step) for i in range(count)])
            step *= 2
    return value


def halving_order(axes):
    order = []
    for axis in axes:
        step = 1
        while step < lax.axis_size(axis):
            order.append((axis, step))
            step *= 2
    return order


def halving_scatter(value, order):
    for axis, step in order:
        count = lax.axis_size(axis)
        index = lax.axis_index(axis)
        half = value.shape[0] // 2
        upper = (index // step) % 2
        keep = lax.dynamic_slice_in_dim(value, upper * half, half, axis=0)
        send = lax.dynamic_slice_in_dim(value, (1 - upper) * half, half, axis=0)
        value = keep + lax.ppermute(send, axis, [(i, i ^ step) for i in range(count)])
    return value


def block_owner(order, blocks):
    owners = []
    sizes = {axis: lax.axis_size(axis) for axis, _ in order}
    for slot in range(blocks):
        coords = {axis: 0 for axis in sizes}
        for position, (axis, step) in enumerate(order):
            if (slot >> (len(order) - 1 - position)) & 1:
                coords[axis] += step
        owner = 0
        for axis in ("rows", "cols"):
            owner = owner * sizes[axis] + coords[axis]
        owners.append(owner)
    return owners


def conv(padded, weights, adjoint):
    if adjoint:
        weights = weights[::-1, ::-1]
    return lax.conv_general_dilated(
        padded,
        weights,
        window_strides=(1, 1),
        padding="VALID",
        dimension_numbers=("NHWC", "HWOI" if adjoint else "HWIO", "NHWC"),
        preferred_element_type=jnp.float32,
    )


def per_device(inputs, upstream, kernel, probe_init):
    batch = inputs.shape[0]
    height = inputs.shape[1]
    breadth = inputs.shape[2]
    channels = kernel.shape[2]
    rows_count = lax.axis_size("rows")
    cols_count = lax.axis_size("cols")
    count = float(height * rows_count * breadth * cols_count * channels)
    field = (("rows", 0), ("cols", 1))
    iterate = probe_init.astype(jnp.bfloat16)
    padded_probe = extended(iterate, field, 2, True)
    back = None
    traces = []
    for iteration in range(ITERS):
        image = conv(padded_probe[None], kernel, False).astype(jnp.bfloat16)
        back = conv(image, kernel, True)[0]
        if iteration + 1 < ITERS:
            padded_back = extended(back, field, 2, True)
            squared = butterfly_sum(jnp.sum(back * back), ("rows", "cols"))
            scale_now = jnp.sqrt(squared / count + 1e-06)
            traces.append(scale_now)
            iterate = (back / scale_now).astype(jnp.bfloat16)
            padded_probe = (padded_back / scale_now).astype(jnp.bfloat16)
    wide_iter = iterate.astype(jnp.float32)
    totals = butterfly_sum(
        jnp.stack([jnp.sum(back * back), jnp.sum(wide_iter * wide_iter)]),
        ("rows", "cols"),
    )
    sum_back = totals[0]
    sum_probe = totals[1]
    norm_trace = jnp.stack(traces)
    lipschitz = jnp.sqrt(jnp.sqrt(sum_back / sum_probe))
    probe_out = back / jnp.sqrt(sum_back / count + 1e-06)
    padded_both = extended(
        jnp.concatenate([inputs, upstream], axis=0), (("rows", 1), ("cols", 2)), 1, False
    )
    padded_in = padded_both[:batch]
    padded_up = padded_both[batch:]
    outputs = conv(padded_in, kernel, False).astype(jnp.bfloat16)
    input_grad = conv(padded_up, kernel, True).astype(jnp.bfloat16)
    order = halving_order(("cols", "rows"))
    blocks = 2 ** len(order)
    width = channels // blocks
    owners = block_owner(order, blocks)
    picked = [owner * width + lane for owner in owners for lane in range(width)]
    local_grad = lax.conv_general_dilated(
        padded_in,
        jnp.take(upstream, jnp.array(picked, dtype=jnp.int32), axis=3),
        window_strides=(1, 1),
        padding="VALID",
        dimension_numbers=("CHWN", "IHWO", "CHWN"),
        preferred_element_type=jnp.float32,
    ).reshape(channels, 9 * channels)
    owned = halving_scatter(local_grad, order)
    owned = butterfly_sum(owned, ("rep",))
    total_cells = batch * lax.axis_size("rep") * height * rows_count * breadth * cols_count
    kernel_grad = owned * (1.0 / math.sqrt(total_cells))
    return (outputs, input_grad, kernel_grad, probe_out, lipschitz, norm_trace)


def solution(mesh):
    placed = (
        P("rep", "rows", "cols", None),
        P("rep", "rows", "cols", None),
        P(),
        P("rows", "cols", None),
    )
    return jax.shard_map(
        per_device,
        mesh=mesh,
        in_specs=placed,
        out_specs=(
            P("rep", "rows", "cols", None),
            P("rep", "rows", "cols", None),
            P(("rows", "cols"), None),
            P("rows", "cols", None),
            P(),
            P(),
        ),
        check_vma=False,
    )
```

```python
import math

import jax
import jax.numpy as jnp
from jax import lax
from jax.sharding import PartitionSpec as P

ITERS = 4


def extended(cells, sides, width, closed):
    for axis, dim in sides:
        count = lax.axis_size(axis)
        ends = count if closed else count - 1
        head = lax.slice_in_dim(cells, 0, width, axis=dim)
        tail = lax.slice_in_dim(cells, cells.shape[dim] - width, cells.shape[dim], axis=dim)
        cells = jnp.concatenate(
            [
                lax.ppermute(tail, axis, [(i, (i + 1) % count) for i in range(ends)]),
                cells,
                lax.ppermute(head, axis, [((i + 1) % count, i) for i in range(ends)]),
            ],
            axis=dim,
        )
    return cells


def butterfly_sum(value, axes):
    for axis in axes:
        count = lax.axis_size(axis)
        step = 1
        while step < count:
            value = value + lax.ppermute(value, axis, [(i, i ^ step) for i in range(count)])
            step *= 2
    return value


def halving_scatter(value, axes):
    for axis in axes:
        count = lax.axis_size(axis)
        index = lax.axis_index(axis)
        step = count // 2
        while step >= 1:
            half = value.shape[0] // 2
            upper = (index // step) % 2
            keep = lax.dynamic_slice_in_dim(value, upper * half, half, axis=0)
            send = lax.dynamic_slice_in_dim(value, (1 - upper) * half, half, axis=0)
            value = keep + lax.ppermute(send, axis, [(i, i ^ step) for i in range(count)])
            step //= 2
    return value


def conv(padded, weights, adjoint):
    if adjoint:
        weights = weights[::-1, ::-1]
    return lax.conv_general_dilated(
        padded,
        weights,
        window_strides=(1, 1),
        padding="VALID",
        dimension_numbers=("NHWC", "HWOI" if adjoint else "HWIO", "NHWC"),
        preferred_element_type=jnp.float32,
    )


def per_device(inputs, upstream, kernel, probe_init):
    batch = inputs.shape[0]
    height = inputs.shape[1]
    breadth = inputs.shape[2]
    channels = kernel.shape[2]
    rows_count = lax.axis_size("rows")
    cols_count = lax.axis_size("cols")
    count = float(height * rows_count * breadth * cols_count * channels)
    padded_both = extended(
        jnp.concatenate([inputs, upstream], axis=0), (("rows", 1), ("cols", 2)), 1, False
    )
    padded_in = padded_both[:batch]
    padded_up = padded_both[batch:]
    outputs = conv(padded_in, kernel, False).astype(jnp.bfloat16)
    input_grad = conv(padded_up, kernel, True).astype(jnp.bfloat16)
    local_grad = lax.conv_general_dilated(
        padded_in,
        upstream,
        window_strides=(1, 1),
        padding="VALID",
        dimension_numbers=("CHWN", "IHWO", "CHWN"),
        preferred_element_type=jnp.float32,
    ).reshape(channels, 9 * channels)
    owned = halving_scatter(local_grad, ("rows", "cols"))
    owned = butterfly_sum(owned, ("rep",))
    field = (("rows", 0), ("cols", 1))
    iterate = probe_init.astype(jnp.bfloat16)
    padded_probe = extended(iterate, field, 2, True)
    back = None
    traces = []
    for iteration in range(ITERS):
        if iteration + 1 == ITERS:
            owned, padded_probe = lax.optimization_barrier((owned, padded_probe))
        image = conv(padded_probe[None], kernel, False).astype(jnp.bfloat16)
        back = conv(image, kernel, True)[0]
        if iteration + 1 < ITERS:
            padded_back = extended(back, field, 2, True)
            squared = butterfly_sum(jnp.sum(back * back), ("rows", "cols"))
            scale_now = jnp.sqrt(squared / count + 1e-06)
            traces.append(scale_now)
            iterate = (back / scale_now).astype(jnp.bfloat16)
            padded_probe = (padded_back / scale_now).astype(jnp.bfloat16)
    wide_iter = iterate.astype(jnp.float32)
    totals = butterfly_sum(
        jnp.stack([jnp.sum(back * back), jnp.sum(wide_iter * wide_iter)]),
        ("rows", "cols"),
    )
    sum_back = totals[0]
    sum_probe = totals[1]
    norm_trace = jnp.stack(traces)
    lipschitz = jnp.sqrt(jnp.sqrt(sum_back / sum_probe))
    probe_out = back / jnp.sqrt(sum_back / count + 1e-06)
    total_cells = batch * lax.axis_size("rep") * height * rows_count * breadth * cols_count
    kernel_grad = owned * (1.0 / math.sqrt(total_cells))
    return (outputs, input_grad, kernel_grad, probe_out, lipschitz, norm_trace)


def solution(mesh):
    placed = (
        P("rep", "rows", "cols", None),
        P("rep", "rows", "cols", None),
        P(),
        P("rows", "cols", None),
    )
    return jax.shard_map(
        per_device,
        mesh=mesh,
        in_specs=placed,
        out_specs=(
            P("rep", "rows", "cols", None),
            P("rep", "rows", "cols", None),
            P(("rows", "cols"), None),
            P("rows", "cols", None),
            P(),
            P(),
        ),
        check_vma=False,
    )
```

```python
import math

import jax
import jax.numpy as jnp
from jax import lax
from jax.sharding import PartitionSpec as P

ITERS = 4


def extended(cells, sides, width, closed):
    for axis, dim in sides:
        count = lax.axis_size(axis)
        ends = count if closed else count - 1
        head = lax.slice_in_dim(cells, 0, width, axis=dim)
        tail = lax.slice_in_dim(cells, cells.shape[dim] - width, cells.shape[dim], axis=dim)
        cells = jnp.concatenate(
            [
                lax.ppermute(tail, axis, [(i, (i + 1) % count) for i in range(ends)]),
                cells,
                lax.ppermute(head, axis, [((i + 1) % count, i) for i in range(ends)]),
            ],
            axis=dim,
        )
    return cells


def butterfly_sum(value, axes):
    for axis in axes:
        count = lax.axis_size(axis)
        step = 1
        while step < count:
            value = value + lax.ppermute(value, axis, [(i, i ^ step) for i in range(count)])
            step *= 2
    return value


def halving_scatter(value, axes):
    for axis in axes:
        count = lax.axis_size(axis)
        index = lax.axis_index(axis)
        step = count // 2
        while step >= 1:
            half = value.shape[0] // 2
            upper = (index // step) % 2
            keep = lax.dynamic_slice_in_dim(value, upper * half, half, axis=0)
            send = lax.dynamic_slice_in_dim(value, (1 - upper) * half, half, axis=0)
            value = keep + lax.ppermute(send, axis, [(i, i ^ step) for i in range(count)])
            step //= 2
    return value


def conv(padded, weights, adjoint):
    if adjoint:
        weights = weights[::-1, ::-1]
    return lax.conv_general_dilated(
        padded,
        weights,
        window_strides=(1, 1),
        padding="VALID",
        dimension_numbers=("NHWC", "HWOI" if adjoint else "HWIO", "NHWC"),
        preferred_element_type=jnp.float32,
    )


def per_device(inputs, upstream, kernel, probe_init):
    batch = inputs.shape[0]
    height = inputs.shape[1]
    breadth = inputs.shape[2]
    channels = kernel.shape[2]
    rows_count = lax.axis_size("rows")
    cols_count = lax.axis_size("cols")
    count = float(height * rows_count * breadth * cols_count * channels)
    field = (("rows", 0), ("cols", 1))
    iterate = probe_init.astype(jnp.bfloat16)
    padded_probe = extended(iterate, field, 2, True)
    back = None
    traces = []
    for iteration in range(ITERS):
        image = conv(padded_probe[None], kernel, False).astype(jnp.bfloat16)
        back = conv(image, kernel, True)[0]
        if iteration + 1 < ITERS:
            row_padded = extended(back, (("rows", 0),), 2, True)
            squared = butterfly_sum(jnp.sum(back * back), ("rows",))
            squared, row_padded = lax.optimization_barrier((squared, row_padded))
            padded_back = extended(row_padded, (("cols", 1),), 2, True)
            squared = butterfly_sum(squared, ("cols",))
            scale_now = jnp.sqrt(squared / count + 1e-06)
            traces.append(scale_now)
            iterate = (back / scale_now).astype(jnp.bfloat16)
            padded_probe = (padded_back / scale_now).astype(jnp.bfloat16)
    wide_iter = iterate.astype(jnp.float32)
    totals = butterfly_sum(
        jnp.stack([jnp.sum(back * back), jnp.sum(wide_iter * wide_iter)]),
        ("rows", "cols"),
    )
    sum_back = totals[0]
    sum_probe = totals[1]
    norm_trace = jnp.stack(traces)
    lipschitz = jnp.sqrt(jnp.sqrt(sum_back / sum_probe))
    probe_out = back / jnp.sqrt(sum_back / count + 1e-06)
    padded_both = extended(
        jnp.concatenate([inputs, upstream], axis=0), (("rows", 1), ("cols", 2)), 1, False
    )
    padded_in = padded_both[:batch]
    padded_up = padded_both[batch:]
    outputs = conv(padded_in, kernel, False).astype(jnp.bfloat16)
    input_grad = conv(padded_up, kernel, True).astype(jnp.bfloat16)
    local_grad = lax.conv_general_dilated(
        padded_up,
        inputs,
        window_strides=(1, 1),
        padding="VALID",
        dimension_numbers=("CHWN", "IHWO", "NHWC"),
        preferred_element_type=jnp.float32,
    )[:, ::-1, ::-1, :].reshape(channels, 9 * channels)
    owned = halving_scatter(local_grad, ("rows", "cols"))
    owned = butterfly_sum(owned, ("rep",))
    total_cells = batch * lax.axis_size("rep") * height * rows_count * breadth * cols_count
    kernel_grad = owned * (1.0 / math.sqrt(total_cells))
    return (outputs, input_grad, kernel_grad, probe_out, lipschitz, norm_trace)


def solution(mesh):
    placed = (
        P("rep", "rows", "cols", None),
        P("rep", "rows", "cols", None),
        P(),
        P("rows", "cols", None),
    )
    return jax.shard_map(
        per_device,
        mesh=mesh,
        in_specs=placed,
        out_specs=(
            P("rep", "rows", "cols", None),
            P("rep", "rows", "cols", None),
            P(("rows", "cols"), None),
            P("rows", "cols", None),
            P(),
            P(),
        ),
        check_vma=False,
    )
```

```python
import math

import jax
import jax.numpy as jnp
from jax import lax
from jax.sharding import PartitionSpec as P

ITERS = 4


def extended(cells, sides, width, closed):
    for axis, dim in sides:
        count = lax.axis_size(axis)
        ends = count if closed else count - 1
        head = lax.slice_in_dim(cells, 0, width, axis=dim)
        tail = lax.slice_in_dim(cells, cells.shape[dim] - width, cells.shape[dim], axis=dim)
        cells = jnp.concatenate(
            [
                lax.ppermute(tail, axis, [(i, (i + 1) % count) for i in range(ends)]),
                cells,
                lax.ppermute(head, axis, [((i + 1) % count, i) for i in range(ends)]),
            ],
            axis=dim,
        )
    return cells


def butterfly_sum(value, axes):
    for axis in axes:
        count = lax.axis_size(axis)
        step = 1
        while step < count:
            value = value + lax.ppermute(value, axis, [(i, i ^ step) for i in range(count)])
            step *= 2
    return value


def halving_scatter(value, axes):
    for axis in axes:
        count = lax.axis_size(axis)
        index = lax.axis_index(axis)
        step = count // 2
        while step >= 1:
            half = value.shape[0] // 2
            upper = (index // step) % 2
            keep = lax.dynamic_slice_in_dim(value, upper * half, half, axis=0)
            send = lax.dynamic_slice_in_dim(value, (1 - upper) * half, half, axis=0)
            value = keep + lax.ppermute(send, axis, [(i, i ^ step) for i in range(count)])
            step //= 2
    return value


def conv(padded, weights, adjoint):
    if adjoint:
        weights = weights[::-1, ::-1]
    return lax.conv_general_dilated(
        padded,
        weights,
        window_strides=(1, 1),
        padding="VALID",
        dimension_numbers=("NHWC", "HWOI" if adjoint else "HWIO", "NHWC"),
        preferred_element_type=jnp.float32,
    )


def per_device(inputs, upstream, kernel, probe_init):
    batch = inputs.shape[0]
    height = inputs.shape[1]
    breadth = inputs.shape[2]
    channels = kernel.shape[2]
    rows_count = lax.axis_size("rows")
    cols_count = lax.axis_size("cols")
    count = float(height * rows_count * breadth * cols_count * channels)
    field = (("rows", 0), ("cols", 1))
    iterate = probe_init.astype(jnp.bfloat16)
    padded_probe = extended(iterate, field, 2, True)

    def power_step(carry, _):
        padded_probe, iterate = carry
        image = conv(padded_probe[None], kernel, False).astype(jnp.bfloat16)
        back = conv(image, kernel, True)[0]
        padded_back = extended(back, field, 2, True)
        squared = butterfly_sum(jnp.sum(back * back), ("rows", "cols"))
        scale_now = jnp.sqrt(squared / count + 1e-06)
        iterate = (back / scale_now).astype(jnp.bfloat16)
        padded_probe = (padded_back / scale_now).astype(jnp.bfloat16)
        return (padded_probe, iterate), scale_now

    (padded_probe, iterate), norm_trace = lax.scan(
        power_step, (padded_probe, iterate), None, length=ITERS - 1
    )
    image = conv(padded_probe[None], kernel, False).astype(jnp.bfloat16)
    back = conv(image, kernel, True)[0]
    wide_iter = iterate.astype(jnp.float32)
    totals = butterfly_sum(
        jnp.stack([jnp.sum(back * back), jnp.sum(wide_iter * wide_iter)]),
        ("rows", "cols"),
    )
    sum_back = totals[0]
    sum_probe = totals[1]
    lipschitz = jnp.sqrt(jnp.sqrt(sum_back / sum_probe))
    probe_out = back / jnp.sqrt(sum_back / count + 1e-06)
    padded_both = extended(
        jnp.concatenate([inputs, upstream], axis=0), (("rows", 1), ("cols", 2)), 1, False
    )
    padded_in = padded_both[:batch]
    padded_up = padded_both[batch:]
    outputs = conv(padded_in, kernel, False).astype(jnp.bfloat16)
    input_grad = conv(padded_up, kernel, True).astype(jnp.bfloat16)
    local_grad = lax.conv_general_dilated(
        padded_in,
        upstream,
        window_strides=(1, 1),
        padding="VALID",
        dimension_numbers=("CHWN", "IHWO", "CHWN"),
        preferred_element_type=jnp.float32,
    ).reshape(channels, 9 * channels)
    owned = halving_scatter(local_grad, ("rows", "cols"))
    owned = butterfly_sum(owned, ("rep",))
    total_cells = batch * lax.axis_size("rep") * height * rows_count * breadth * cols_count
    kernel_grad = owned * (1.0 / math.sqrt(total_cells))
    return (outputs, input_grad, kernel_grad, probe_out, lipschitz, norm_trace)


def solution(mesh):
    placed = (
        P("rep", "rows", "cols", None),
        P("rep", "rows", "cols", None),
        P(),
        P("rows", "cols", None),
    )
    return jax.shard_map(
        per_device,
        mesh=mesh,
        in_specs=placed,
        out_specs=(
            P("rep", "rows", "cols", None),
            P("rep", "rows", "cols", None),
            P(("rows", "cols"), None),
            P("rows", "cols", None),
            P(),
            P(),
        ),
        check_vma=False,
    )
```

```python
import math

import jax
import jax.numpy as jnp
from jax import lax
from jax.sharding import PartitionSpec as P

ITERS = 4


def extended(cells, sides, width, closed):
    for axis, dim in sides:
        count = lax.axis_size(axis)
        ends = count if closed else count - 1
        head = lax.slice_in_dim(cells, 0, width, axis=dim)
        tail = lax.slice_in_dim(cells, cells.shape[dim] - width, cells.shape[dim], axis=dim)
        cells = jnp.concatenate(
            [
                lax.ppermute(tail, axis, [(i, (i + 1) % count) for i in range(ends)]),
                cells,
                lax.ppermute(head, axis, [((i + 1) % count, i) for i in range(ends)]),
            ],
            axis=dim,
        )
    return cells


def butterfly_sum(value, axes):
    for axis in axes:
        count = lax.axis_size(axis)
        step = 1
        while step < count:
            value = value + lax.ppermute(value, axis, [(i, i ^ step) for i in range(count)])
            step *= 2
    return value


def halving_order(axes):
    order = []
    for axis in axes:
        step = 1
        while step < lax.axis_size(axis):
            order.append((axis, step))
            step *= 2
    return order


def halving_scatter(value, order):
    for axis, step in order:
        count = lax.axis_size(axis)
        index = lax.axis_index(axis)
        half = value.shape[0] // 2
        upper = (index // step) % 2
        keep = lax.dynamic_slice_in_dim(value, upper * half, half, axis=0)
        send = lax.dynamic_slice_in_dim(value, (1 - upper) * half, half, axis=0)
        value = keep + lax.ppermute(send, axis, [(i, i ^ step) for i in range(count)])
    return value


def conv(padded, weights, adjoint):
    if adjoint:
        weights = weights[::-1, ::-1]
    return lax.conv_general_dilated(
        padded,
        weights,
        window_strides=(1, 1),
        padding="VALID",
        dimension_numbers=("NHWC", "HWOI" if adjoint else "HWIO", "NHWC"),
        preferred_element_type=jnp.float32,
    )


def per_device(inputs, upstream, kernel, probe_init):
    batch = inputs.shape[0]
    height = inputs.shape[1]
    breadth = inputs.shape[2]
    channels = kernel.shape[2]
    rows_count = lax.axis_size("rows")
    cols_count = lax.axis_size("cols")
    count = float(height * rows_count * breadth * cols_count * channels)
    field = (("rows", 0), ("cols", 1))
    iterate = probe_init.astype(jnp.bfloat16)
    padded_probe = extended(iterate, field, 2, True)

    def power_step(carry, _):
        padded_probe, iterate = carry
        image = conv(padded_probe[None], kernel, False).astype(jnp.bfloat16)
        back = conv(image, kernel, True)[0]
        padded_back = extended(back, field, 2, True)
        squared = butterfly_sum(jnp.sum(back * back), ("rows", "cols"))
        scale_now = jnp.sqrt(squared / count + 1e-06)
        iterate = (back / scale_now).astype(jnp.bfloat16)
        padded_probe = (padded_back / scale_now).astype(jnp.bfloat16)
        return (padded_probe, iterate), scale_now

    (padded_probe, iterate), norm_trace = lax.scan(
        power_step, (padded_probe, iterate), None, length=ITERS - 1
    )
    image = conv(padded_probe[None], kernel, False).astype(jnp.bfloat16)
    back = conv(image, kernel, True)[0]
    wide_iter = iterate.astype(jnp.float32)
    totals = butterfly_sum(
        jnp.stack([jnp.sum(back * back), jnp.sum(wide_iter * wide_iter)]),
        ("rows", "cols"),
    )
    sum_back = totals[0]
    sum_probe = totals[1]
    lipschitz = jnp.sqrt(jnp.sqrt(sum_back / sum_probe))
    probe_out = back / jnp.sqrt(sum_back / count + 1e-06)
    padded_both = extended(
        jnp.concatenate([inputs, upstream], axis=0), (("rows", 1), ("cols", 2)), 1, False
    )
    padded_in = padded_both[:batch]
    padded_up = padded_both[batch:]
    outputs = conv(padded_in, kernel, False).astype(jnp.bfloat16)
    input_grad = conv(padded_up, kernel, True).astype(jnp.bfloat16)
    local_grad = lax.conv_general_dilated(
        padded_in,
        upstream,
        window_strides=(1, 1),
        padding="VALID",
        dimension_numbers=("CHWN", "IHWO", "CHWN"),
        preferred_element_type=jnp.float32,
    ).reshape(channels, 9 * channels)
    order = halving_order(("cols", "rows"))
    bits = len(order)
    local_grad = local_grad.reshape((2,) * bits + (channels >> bits, 9 * channels))
    local_grad = local_grad.transpose(tuple(reversed(range(bits))) + (bits, bits + 1))
    owned = halving_scatter(local_grad.reshape(channels, 9 * channels), order)
    owned = butterfly_sum(owned, ("rep",))
    total_cells = batch * lax.axis_size("rep") * height * rows_count * breadth * cols_count
    kernel_grad = owned * (1.0 / math.sqrt(total_cells))
    return (outputs, input_grad, kernel_grad, probe_out, lipschitz, norm_trace)


def solution(mesh):
    placed = (
        P("rep", "rows", "cols", None),
        P("rep", "rows", "cols", None),
        P(),
        P("rows", "cols", None),
    )
    return jax.shard_map(
        per_device,
        mesh=mesh,
        in_specs=placed,
        out_specs=(
            P("rep", "rows", "cols", None),
            P("rep", "rows", "cols", None),
            P(("rows", "cols"), None),
            P("rows", "cols", None),
            P(),
            P(),
        ),
        check_vma=False,
    )
```

```python
import math

import jax
import jax.numpy as jnp
from jax import lax
from jax.sharding import PartitionSpec as P

ITERS = 4


def extended(cells, sides, width, closed):
    for axis, dim in sides:
        count = lax.axis_size(axis)
        ends = count if closed else count - 1
        head = lax.slice_in_dim(cells, 0, width, axis=dim)
        tail = lax.slice_in_dim(cells, cells.shape[dim] - width, cells.shape[dim], axis=dim)
        cells = jnp.concatenate(
            [
                lax.ppermute(tail, axis, [(i, (i + 1) % count) for i in range(ends)]),
                cells,
                lax.ppermute(head, axis, [((i + 1) % count, i) for i in range(ends)]),
            ],
            axis=dim,
        )
    return cells


def butterfly_sum(value, axes):
    for axis in axes:
        count = lax.axis_size(axis)
        step = 1
        while step < count:
            value = value + lax.ppermute(value, axis, [(i, i ^ step) for i in range(count)])
            step *= 2
    return value


def halving_scatter(value, axes):
    for axis in axes:
        count = lax.axis_size(axis)
        index = lax.axis_index(axis)
        step = count // 2
        while step >= 1:
            half = value.shape[0] // 2
            upper = (index // step) % 2
            keep = lax.dynamic_slice_in_dim(value, upper * half, half, axis=0)
            send = lax.dynamic_slice_in_dim(value, (1 - upper) * half, half, axis=0)
            value = keep + lax.ppermute(send, axis, [(i, i ^ step) for i in range(count)])
            step //= 2
    return value


def conv(padded, weights, adjoint):
    if adjoint:
        weights = weights[::-1, ::-1]
    return lax.conv_general_dilated(
        padded,
        weights,
        window_strides=(1, 1),
        padding="VALID",
        dimension_numbers=("NHWC", "HWOI" if adjoint else "HWIO", "NHWC"),
        preferred_element_type=jnp.float32,
    )


def per_device(inputs, upstream, kernel, probe_init):
    batch = inputs.shape[0]
    height = inputs.shape[1]
    breadth = inputs.shape[2]
    channels = kernel.shape[2]
    rows_count = lax.axis_size("rows")
    cols_count = lax.axis_size("cols")
    count = float(height * rows_count * breadth * cols_count * channels)
    field = (("rows", 0), ("cols", 1))
    iterate = probe_init.astype(jnp.bfloat16)
    padded_probe = extended(iterate, field, 2, True)

    def power_step(carry, _):
        padded_probe, iterate = carry
        image = conv(padded_probe[None], kernel, False).astype(jnp.bfloat16)
        back = conv(image, kernel, True)[0]
        row_padded = extended(back, field[:1], 2, True)
        squared = butterfly_sum(jnp.sum(back * back), ("rows",))
        squared, row_padded = lax.optimization_barrier((squared, row_padded))
        padded_back = extended(row_padded, field[1:], 2, True)
        squared = butterfly_sum(squared, ("cols",))
        scale_now = jnp.sqrt(squared / count + 1e-06)
        iterate = (back / scale_now).astype(jnp.bfloat16)
        padded_probe = (padded_back / scale_now).astype(jnp.bfloat16)
        return (padded_probe, iterate), scale_now

    (padded_probe, iterate), norm_trace = lax.scan(
        power_step, (padded_probe, iterate), None, length=ITERS - 1
    )
    image = conv(padded_probe[None], kernel, False).astype(jnp.bfloat16)
    back = conv(image, kernel, True)[0]
    wide_iter = iterate.astype(jnp.float32)
    totals = butterfly_sum(
        jnp.stack([jnp.sum(back * back), jnp.sum(wide_iter * wide_iter)]),
        ("rows", "cols"),
    )
    sum_back = totals[0]
    sum_probe = totals[1]
    lipschitz = jnp.sqrt(jnp.sqrt(sum_back / sum_probe))
    probe_out = back / jnp.sqrt(sum_back / count + 1e-06)
    padded_both = extended(
        jnp.concatenate([inputs, upstream], axis=0), (("rows", 1), ("cols", 2)), 1, False
    )
    padded_in = padded_both[:batch]
    padded_up = padded_both[batch:]
    outputs = conv(padded_in, kernel, False).astype(jnp.bfloat16)
    input_grad = conv(padded_up, kernel, True).astype(jnp.bfloat16)
    local_grad = lax.conv_general_dilated(
        padded_in,
        upstream,
        window_strides=(1, 1),
        padding="VALID",
        dimension_numbers=("CHWN", "IHWO", "CHWN"),
        preferred_element_type=jnp.float32,
    ).reshape(channels, 9 * channels)
    owned = halving_scatter(local_grad, ("rows", "cols"))
    owned = butterfly_sum(owned, ("rep",))
    total_cells = batch * lax.axis_size("rep") * height * rows_count * breadth * cols_count
    kernel_grad = owned * (1.0 / math.sqrt(total_cells))
    return (outputs, input_grad, kernel_grad, probe_out, lipschitz, norm_trace)


def solution(mesh):
    placed = (
        P("rep", "rows", "cols", None),
        P("rep", "rows", "cols", None),
        P(),
        P("rows", "cols", None),
    )
    return jax.shard_map(
        per_device,
        mesh=mesh,
        in_specs=placed,
        out_specs=(
            P("rep", "rows", "cols", None),
            P("rep", "rows", "cols", None),
            P(("rows", "cols"), None),
            P("rows", "cols", None),
            P(),
            P(),
        ),
        check_vma=False,
    )
```

```python
import math

import jax
import jax.numpy as jnp
from jax import lax
from jax.sharding import PartitionSpec as P

ITERS = 4


def extended(cells, sides, width, closed):
    for axis, dim in sides:
        count = lax.axis_size(axis)
        ends = count if closed else count - 1
        head = lax.slice_in_dim(cells, 0, width, axis=dim)
        tail = lax.slice_in_dim(cells, cells.shape[dim] - width, cells.shape[dim], axis=dim)
        cells = jnp.concatenate(
            [
                lax.ppermute(tail, axis, [(i, (i + 1) % count) for i in range(ends)]),
                cells,
                lax.ppermute(head, axis, [((i + 1) % count, i) for i in range(ends)]),
            ],
            axis=dim,
        )
    return cells


def butterfly_sum(value, axes):
    for axis in axes:
        count = lax.axis_size(axis)
        step = 1
        while step < count:
            value = value + lax.ppermute(value, axis, [(i, i ^ step) for i in range(count)])
            step *= 2
    return value


def halving_scatter(value, axes):
    for axis in axes:
        count = lax.axis_size(axis)
        index = lax.axis_index(axis)
        step = count // 2
        while step >= 1:
            half = value.shape[0] // 2
            upper = (index // step) % 2
            keep = lax.dynamic_slice_in_dim(value, upper * half, half, axis=0)
            send = lax.dynamic_slice_in_dim(value, (1 - upper) * half, half, axis=0)
            value = keep + lax.ppermute(send, axis, [(i, i ^ step) for i in range(count)])
            step //= 2
    return value


def conv(padded, weights, adjoint):
    if adjoint:
        weights = weights[::-1, ::-1]
    return lax.conv_general_dilated(
        padded,
        weights,
        window_strides=(1, 1),
        padding="VALID",
        dimension_numbers=("NHWC", "HWOI" if adjoint else "HWIO", "NHWC"),
        preferred_element_type=jnp.float32,
    )


def per_device(inputs, upstream, kernel, probe_init):
    batch = inputs.shape[0]
    height = inputs.shape[1]
    breadth = inputs.shape[2]
    channels = kernel.shape[2]
    rows_count = lax.axis_size("rows")
    cols_count = lax.axis_size("cols")
    count = float(height * rows_count * breadth * cols_count * channels)
    field = (("rows", 0), ("cols", 1))
    iterate = probe_init.astype(jnp.bfloat16)
    padded_probe = extended(iterate, field, 2, True)

    def power_step(carry, _):
        padded_probe, iterate = carry
        image = conv(padded_probe[None], kernel, False).astype(jnp.bfloat16)
        back = conv(image, kernel, True)[0]
        row_padded = extended(back, field[:1], 2, True)
        squared = butterfly_sum(jnp.sum(back * back), ("rows",))
        squared, row_padded = lax.optimization_barrier((squared, row_padded))
        padded_back = extended(row_padded, field[1:], 2, True)
        squared = butterfly_sum(squared, ("cols",))
        scale_now = jnp.sqrt(squared / count + 1e-06)
        iterate = (back / scale_now).astype(jnp.bfloat16)
        padded_probe = (padded_back / scale_now).astype(jnp.bfloat16)
        return (padded_probe, iterate), scale_now

    padded_both = extended(
        jnp.concatenate([inputs, upstream], axis=0), (("rows", 1), ("cols", 2)), 1, False
    )
    padded_in = padded_both[:batch]
    padded_up = padded_both[batch:]
    outputs = conv(padded_in, kernel, False).astype(jnp.bfloat16)
    input_grad = conv(padded_up, kernel, True).astype(jnp.bfloat16)
    local_grad = lax.conv_general_dilated(
        padded_in,
        upstream,
        window_strides=(1, 1),
        padding="VALID",
        dimension_numbers=("CHWN", "IHWO", "CHWN"),
        preferred_element_type=jnp.float32,
    ).reshape(channels, 9 * channels)
    owned = halving_scatter(local_grad, ("rows",))
    owned, padded_probe = lax.optimization_barrier((owned, padded_probe))
    (padded_probe, iterate), norm_trace = lax.scan(
        power_step, (padded_probe, iterate), None, length=ITERS - 1
    )
    image = conv(padded_probe[None], kernel, False).astype(jnp.bfloat16)
    back = conv(image, kernel, True)[0]
    wide_iter = iterate.astype(jnp.float32)
    totals = butterfly_sum(
        jnp.stack([jnp.sum(back * back), jnp.sum(wide_iter * wide_iter)]),
        ("rows", "cols"),
    )
    sum_back = totals[0]
    sum_probe = totals[1]
    lipschitz = jnp.sqrt(jnp.sqrt(sum_back / sum_probe))
    probe_out = back / jnp.sqrt(sum_back / count + 1e-06)
    owned = halving_scatter(owned, ("cols",))
    owned = butterfly_sum(owned, ("rep",))
    total_cells = batch * lax.axis_size("rep") * height * rows_count * breadth * cols_count
    kernel_grad = owned * (1.0 / math.sqrt(total_cells))
    return (outputs, input_grad, kernel_grad, probe_out, lipschitz, norm_trace)


def solution(mesh):
    placed = (
        P("rep", "rows", "cols", None),
        P("rep", "rows", "cols", None),
        P(),
        P("rows", "cols", None),
    )
    return jax.shard_map(
        per_device,
        mesh=mesh,
        in_specs=placed,
        out_specs=(
            P("rep", "rows", "cols", None),
            P("rep", "rows", "cols", None),
            P(("rows", "cols"), None),
            P("rows", "cols", None),
            P(),
            P(),
        ),
        check_vma=False,
    )
```

```python
import math

import jax
import jax.numpy as jnp
from jax import lax
from jax.sharding import PartitionSpec as P

ITERS = 4


def extended(cells, sides, width, closed):
    for axis, dim in sides:
        count = lax.axis_size(axis)
        ends = count if closed else count - 1
        head = lax.slice_in_dim(cells, 0, width, axis=dim)
        tail = lax.slice_in_dim(cells, cells.shape[dim] - width, cells.shape[dim], axis=dim)
        cells = jnp.concatenate(
            [
                lax.ppermute(tail, axis, [(i, (i + 1) % count) for i in range(ends)]),
                cells,
                lax.ppermute(head, axis, [((i + 1) % count, i) for i in range(ends)]),
            ],
            axis=dim,
        )
    return cells


def butterfly_sum(value, axes):
    for axis in axes:
        count = lax.axis_size(axis)
        step = 1
        while step < count:
            value = value + lax.ppermute(value, axis, [(i, i ^ step) for i in range(count)])
            step *= 2
    return value


def halving_scatter(value, axes):
    for axis in axes:
        count = lax.axis_size(axis)
        index = lax.axis_index(axis)
        step = count // 2
        while step >= 1:
            half = value.shape[0] // 2
            upper = (index // step) % 2
            keep = lax.dynamic_slice_in_dim(value, upper * half, half, axis=0)
            send = lax.dynamic_slice_in_dim(value, (1 - upper) * half, half, axis=0)
            value = keep + lax.ppermute(send, axis, [(i, i ^ step) for i in range(count)])
            step //= 2
    return value


def conv(padded, weights, adjoint):
    if adjoint:
        weights = weights[::-1, ::-1]
    return lax.conv_general_dilated(
        padded,
        weights,
        window_strides=(1, 1),
        padding="VALID",
        dimension_numbers=("NHWC", "HWOI" if adjoint else "HWIO", "NHWC"),
        preferred_element_type=jnp.float32,
    )


def per_device(inputs, upstream, kernel, probe_init):
    batch = inputs.shape[0]
    height = inputs.shape[1]
    breadth = inputs.shape[2]
    channels = kernel.shape[2]
    rows_count = lax.axis_size("rows")
    cols_count = lax.axis_size("cols")
    count = float(height * rows_count * breadth * cols_count * channels)
    field = (("rows", 0), ("cols", 1))
    iterate = probe_init.astype(jnp.bfloat16)
    padded_probe = extended(iterate, field, 2, True)

    def power_step(carry, _):
        padded_probe, iterate = carry
        image = conv(padded_probe[None], kernel, False).astype(jnp.bfloat16)
        back = conv(image, kernel, True)[0]
        row_padded = extended(back, field[:1], 2, True)
        squared = butterfly_sum(jnp.sum(back * back), ("rows",))
        squared, row_padded = lax.optimization_barrier((squared, row_padded))
        padded_back = extended(row_padded, field[1:], 2, True)
        squared = butterfly_sum(squared, ("cols",))
        scale_now = jnp.sqrt(squared / count + 1e-06)
        iterate = (back / scale_now).astype(jnp.bfloat16)
        padded_probe = (padded_back / scale_now).astype(jnp.bfloat16)
        return (padded_probe, iterate), scale_now

    padded_both = extended(
        jnp.concatenate([inputs, upstream], axis=0), (("rows", 1), ("cols", 2)), 1, False
    )
    padded_in = padded_both[:batch]
    padded_up = padded_both[batch:]
    outputs = conv(padded_in, kernel, False).astype(jnp.bfloat16)
    input_grad = conv(padded_up, kernel, True).astype(jnp.bfloat16)
    local_grad = lax.conv_general_dilated(
        padded_in,
        upstream,
        window_strides=(1, 1),
        padding="VALID",
        dimension_numbers=("CHWN", "IHWO", "CHWN"),
        preferred_element_type=jnp.float32,
    ).reshape(channels, 9 * channels)
    local_grad, outputs, input_grad, padded_probe = lax.optimization_barrier(
        (local_grad, outputs, input_grad, padded_probe)
    )
    (padded_probe, iterate), norm_trace = lax.scan(
        power_step, (padded_probe, iterate), None, length=ITERS - 1
    )
    image = conv(padded_probe[None], kernel, False).astype(jnp.bfloat16)
    back = conv(image, kernel, True)[0]
    wide_iter = iterate.astype(jnp.float32)
    totals = butterfly_sum(
        jnp.stack([jnp.sum(back * back), jnp.sum(wide_iter * wide_iter)]),
        ("rows", "cols"),
    )
    sum_back = totals[0]
    sum_probe = totals[1]
    lipschitz = jnp.sqrt(jnp.sqrt(sum_back / sum_probe))
    probe_out = back / jnp.sqrt(sum_back / count + 1e-06)
    owned = halving_scatter(local_grad, ("rows", "cols"))
    owned = butterfly_sum(owned, ("rep",))
    total_cells = batch * lax.axis_size("rep") * height * rows_count * breadth * cols_count
    kernel_grad = owned * (1.0 / math.sqrt(total_cells))
    return (outputs, input_grad, kernel_grad, probe_out, lipschitz, norm_trace)


def solution(mesh):
    placed = (
        P("rep", "rows", "cols", None),
        P("rep", "rows", "cols", None),
        P(),
        P("rows", "cols", None),
    )
    return jax.shard_map(
        per_device,
        mesh=mesh,
        in_specs=placed,
        out_specs=(
            P("rep", "rows", "cols", None),
            P("rep", "rows", "cols", None),
            P(("rows", "cols"), None),
            P("rows", "cols", None),
            P(),
            P(),
        ),
        check_vma=False,
    )
```

```python
import math

import jax
import jax.numpy as jnp
from jax import lax
from jax.sharding import PartitionSpec as P

ITERS = 4


def extended(cells, sides, width, closed):
    for axis, dim in sides:
        count = lax.axis_size(axis)
        ends = count if closed else count - 1
        head = lax.slice_in_dim(cells, 0, width, axis=dim)
        tail = lax.slice_in_dim(cells, cells.shape[dim] - width, cells.shape[dim], axis=dim)
        cells = jnp.concatenate(
            [
                lax.ppermute(tail, axis, [(i, (i + 1) % count) for i in range(ends)]),
                cells,
                lax.ppermute(head, axis, [((i + 1) % count, i) for i in range(ends)]),
            ],
            axis=dim,
        )
    return cells


def butterfly_sum(value, axes):
    for axis in axes:
        count = lax.axis_size(axis)
        step = 1
        while step < count:
            value = value + lax.ppermute(value, axis, [(i, i ^ step) for i in range(count)])
            step *= 2
    return value


def halving_order(axes):
    order = []
    for axis in axes:
        step = 1
        while step < lax.axis_size(axis):
            order.append((axis, step))
            step *= 2
    return order


def halving_scatter(value, order):
    for axis, step in order:
        count = lax.axis_size(axis)
        index = lax.axis_index(axis)
        half = value.shape[0] // 2
        upper = (index // step) % 2
        keep = lax.dynamic_slice_in_dim(value, upper * half, half, axis=0)
        send = lax.dynamic_slice_in_dim(value, (1 - upper) * half, half, axis=0)
        value = keep + lax.ppermute(send, axis, [(i, i ^ step) for i in range(count)])
    return value


def conv(padded, weights, adjoint):
    if adjoint:
        weights = weights[::-1, ::-1]
    return lax.conv_general_dilated(
        padded,
        weights,
        window_strides=(1, 1),
        padding="VALID",
        dimension_numbers=("NHWC", "HWOI" if adjoint else "HWIO", "NHWC"),
        preferred_element_type=jnp.float32,
    )


def per_device(inputs, upstream, kernel, probe_init):
    batch = inputs.shape[0]
    height = inputs.shape[1]
    breadth = inputs.shape[2]
    channels = kernel.shape[2]
    rows_count = lax.axis_size("rows")
    cols_count = lax.axis_size("cols")
    count = float(height * rows_count * breadth * cols_count * channels)
    field = (("rows", 0), ("cols", 1))
    iterate = probe_init.astype(jnp.bfloat16)
    padded_probe = extended(iterate, field, 2, True)

    def power_step(carry, _):
        padded_probe, iterate = carry
        image = conv(padded_probe[None], kernel, False).astype(jnp.bfloat16)
        back = conv(image, kernel, True)[0]
        row_padded = extended(back, field[:1], 2, True)
        squared = butterfly_sum(jnp.sum(back * back), ("rows",))
        squared, row_padded = lax.optimization_barrier((squared, row_padded))
        padded_back = extended(row_padded, field[1:], 2, True)
        squared = butterfly_sum(squared, ("cols",))
        scale_now = jnp.sqrt(squared / count + 1e-06)
        iterate = (back / scale_now).astype(jnp.bfloat16)
        padded_probe = (padded_back / scale_now).astype(jnp.bfloat16)
        return (padded_probe, iterate), scale_now

    padded_both = extended(
        jnp.concatenate([inputs, upstream], axis=0), (("rows", 1), ("cols", 2)), 1, False
    )
    padded_in = padded_both[:batch]
    padded_up = padded_both[batch:]
    outputs = conv(padded_in, kernel, False).astype(jnp.bfloat16)
    input_grad = conv(padded_up, kernel, True).astype(jnp.bfloat16)
    local_grad = lax.conv_general_dilated(
        padded_in,
        upstream,
        window_strides=(1, 1),
        padding="VALID",
        dimension_numbers=("CHWN", "IHWO", "CHWN"),
        preferred_element_type=jnp.float32,
    ).reshape(channels, 9 * channels)
    order = halving_order(("cols", "rows"))
    bits = len(order)
    local_grad = local_grad.reshape((2,) * bits + (channels >> bits, 9 * channels))
    local_grad = local_grad.transpose(tuple(reversed(range(bits))) + (bits, bits + 1))
    local_grad, outputs, input_grad, padded_probe = lax.optimization_barrier(
        (local_grad, outputs, input_grad, padded_probe)
    )
    (padded_probe, iterate), norm_trace = lax.scan(
        power_step, (padded_probe, iterate), None, length=ITERS - 1
    )
    image = conv(padded_probe[None], kernel, False).astype(jnp.bfloat16)
    back = conv(image, kernel, True)[0]
    wide_iter = iterate.astype(jnp.float32)
    totals = butterfly_sum(
        jnp.stack([jnp.sum(back * back), jnp.sum(wide_iter * wide_iter)]),
        ("rows", "cols"),
    )
    sum_back = totals[0]
    sum_probe = totals[1]
    lipschitz = jnp.sqrt(jnp.sqrt(sum_back / sum_probe))
    probe_out = back / jnp.sqrt(sum_back / count + 1e-06)
    owned = halving_scatter(local_grad.reshape(channels, 9 * channels), order)
    owned = butterfly_sum(owned, ("rep",))
    total_cells = batch * lax.axis_size("rep") * height * rows_count * breadth * cols_count
    kernel_grad = owned * (1.0 / math.sqrt(total_cells))
    return (outputs, input_grad, kernel_grad, probe_out, lipschitz, norm_trace)


def solution(mesh):
    placed = (
        P("rep", "rows", "cols", None),
        P("rep", "rows", "cols", None),
        P(),
        P("rows", "cols", None),
    )
    return jax.shard_map(
        per_device,
        mesh=mesh,
        in_specs=placed,
        out_specs=(
            P("rep", "rows", "cols", None),
            P("rep", "rows", "cols", None),
            P(("rows", "cols"), None),
            P("rows", "cols", None),
            P(),
            P(),
        ),
        check_vma=False,
    )
```

```python
import math

import jax
import jax.numpy as jnp
from jax import lax
from jax.sharding import PartitionSpec as P

ITERS = 4


def extended(cells, sides, width, closed):
    for axis, dim in sides:
        count = lax.axis_size(axis)
        ends = count if closed else count - 1
        head = lax.slice_in_dim(cells, 0, width, axis=dim)
        tail = lax.slice_in_dim(cells, cells.shape[dim] - width, cells.shape[dim], axis=dim)
        cells = jnp.concatenate(
            [
                lax.ppermute(tail, axis, [(i, (i + 1) % count) for i in range(ends)]),
                cells,
                lax.ppermute(head, axis, [((i + 1) % count, i) for i in range(ends)]),
            ],
            axis=dim,
        )
    return cells


def butterfly_sum(value, axes):
    for axis in axes:
        count = lax.axis_size(axis)
        step = 1
        while step < count:
            value = value + lax.ppermute(value, axis, [(i, i ^ step) for i in range(count)])
            step *= 2
    return value


def halving_scatter(value, axes):
    for axis in axes:
        count = lax.axis_size(axis)
        index = lax.axis_index(axis)
        step = count // 2
        while step >= 1:
            half = value.shape[0] // 2
            upper = (index // step) % 2
            keep = lax.dynamic_slice_in_dim(value, upper * half, half, axis=0)
            send = lax.dynamic_slice_in_dim(value, (1 - upper) * half, half, axis=0)
            value = keep + lax.ppermute(send, axis, [(i, i ^ step) for i in range(count)])
            step //= 2
    return value


def conv(padded, weights, adjoint):
    if adjoint:
        weights = weights[::-1, ::-1]
    return lax.conv_general_dilated(
        padded,
        weights,
        window_strides=(1, 1),
        padding="VALID",
        dimension_numbers=("NHWC", "HWOI" if adjoint else "HWIO", "NHWC"),
        preferred_element_type=jnp.float32,
    )


def per_device(inputs, upstream, kernel, probe_init):
    batch = inputs.shape[0]
    height = inputs.shape[1]
    breadth = inputs.shape[2]
    channels = kernel.shape[2]
    rows_count = lax.axis_size("rows")
    cols_count = lax.axis_size("cols")
    count = float(height * rows_count * breadth * cols_count * channels)
    field = (("rows", 0), ("cols", 1))
    iterate = probe_init.astype(jnp.bfloat16)
    padded_probe = extended(iterate, field, 2, True)

    def power_step(carry, _):
        padded_probe, iterate = carry
        image = conv(padded_probe[None], kernel, False).astype(jnp.bfloat16)
        back = conv(image, kernel, True)[0]
        row_padded = extended(back, field[:1], 2, True)
        squared = butterfly_sum(jnp.sum(back * back), ("rows",))
        squared, row_padded = lax.optimization_barrier((squared, row_padded))
        padded_back = extended(row_padded, field[1:], 2, True)
        squared = butterfly_sum(squared, ("cols",))
        scale_now = jnp.sqrt(squared / count + 1e-06)
        iterate = (back / scale_now).astype(jnp.bfloat16)
        padded_probe = (padded_back / scale_now).astype(jnp.bfloat16)
        return (padded_probe, iterate), scale_now

    padded_both = extended(
        jnp.concatenate([inputs, upstream], axis=0), (("rows", 1), ("cols", 2)), 1, False
    )
    padded_in = padded_both[:batch]
    padded_up = padded_both[batch:]
    outputs = conv(padded_in, kernel, False).astype(jnp.bfloat16)
    input_grad = conv(padded_up, kernel, True).astype(jnp.bfloat16)
    local_grad = lax.conv_general_dilated(
        padded_in,
        upstream,
        window_strides=(1, 1),
        padding="VALID",
        dimension_numbers=("CHWN", "IHWO", "CHWN"),
        preferred_element_type=jnp.float32,
    ).reshape(channels, 9 * channels)
    local_grad, outputs, input_grad, padded_probe = lax.optimization_barrier(
        (local_grad, outputs, input_grad, padded_probe)
    )
    (padded_probe, iterate), norm_trace = lax.scan(
        power_step, (padded_probe, iterate), None, length=ITERS - 1
    )
    local_grad, padded_probe = lax.optimization_barrier((local_grad, padded_probe))
    image = conv(padded_probe[None], kernel, False).astype(jnp.bfloat16)
    back = conv(image, kernel, True)[0]
    wide_iter = iterate.astype(jnp.float32)
    totals = butterfly_sum(
        jnp.stack([jnp.sum(back * back), jnp.sum(wide_iter * wide_iter)]),
        ("rows", "cols"),
    )
    sum_back = totals[0]
    sum_probe = totals[1]
    lipschitz = jnp.sqrt(jnp.sqrt(sum_back / sum_probe))
    probe_out = back / jnp.sqrt(sum_back / count + 1e-06)
    owned = halving_scatter(local_grad, ("rows", "cols"))
    owned = butterfly_sum(owned, ("rep",))
    total_cells = batch * lax.axis_size("rep") * height * rows_count * breadth * cols_count
    kernel_grad = owned * (1.0 / math.sqrt(total_cells))
    return (outputs, input_grad, kernel_grad, probe_out, lipschitz, norm_trace)


def solution(mesh):
    placed = (
        P("rep", "rows", "cols", None),
        P("rep", "rows", "cols", None),
        P(),
        P("rows", "cols", None),
    )
    return jax.shard_map(
        per_device,
        mesh=mesh,
        in_specs=placed,
        out_specs=(
            P("rep", "rows", "cols", None),
            P("rep", "rows", "cols", None),
            P(("rows", "cols"), None),
            P("rows", "cols", None),
            P(),
            P(),
        ),
        check_vma=False,
    )
```

```python
import math

import jax
import jax.numpy as jnp
from jax import lax
from jax.sharding import PartitionSpec as P

ITERS = 4


def extended(cells, sides, width, closed):
    for axis, dim in sides:
        count = lax.axis_size(axis)
        ends = count if closed else count - 1
        head = lax.slice_in_dim(cells, 0, width, axis=dim)
        tail = lax.slice_in_dim(cells, cells.shape[dim] - width, cells.shape[dim], axis=dim)
        cells = jnp.concatenate(
            [
                lax.ppermute(tail, axis, [(i, (i + 1) % count) for i in range(ends)]),
                cells,
                lax.ppermute(head, axis, [((i + 1) % count, i) for i in range(ends)]),
            ],
            axis=dim,
        )
    return cells


def butterfly_sum(value, axes):
    for axis in axes:
        count = lax.axis_size(axis)
        step = 1
        while step < count:
            value = value + lax.ppermute(value, axis, [(i, i ^ step) for i in range(count)])
            step *= 2
    return value


def halving_scatter(value, axes):
    for axis in axes:
        count = lax.axis_size(axis)
        index = lax.axis_index(axis)
        step = count // 2
        while step >= 1:
            half = value.shape[0] // 2
            upper = (index // step) % 2
            keep = lax.dynamic_slice_in_dim(value, upper * half, half, axis=0)
            send = lax.dynamic_slice_in_dim(value, (1 - upper) * half, half, axis=0)
            if send.size * 4 > 256 * 2304:
                send = send.astype(jnp.bfloat16)
            received = lax.ppermute(send, axis, [(i, i ^ step) for i in range(count)])
            value = keep + received.astype(jnp.float32)
            step //= 2
    return value


def conv(padded, weights, adjoint):
    if adjoint:
        weights = weights[::-1, ::-1]
    return lax.conv_general_dilated(
        padded,
        weights,
        window_strides=(1, 1),
        padding="VALID",
        dimension_numbers=("NHWC", "HWOI" if adjoint else "HWIO", "NHWC"),
        preferred_element_type=jnp.float32,
    )


def per_device(inputs, upstream, kernel, probe_init):
    batch = inputs.shape[0]
    height = inputs.shape[1]
    breadth = inputs.shape[2]
    channels = kernel.shape[2]
    rows_count = lax.axis_size("rows")
    cols_count = lax.axis_size("cols")
    count = float(height * rows_count * breadth * cols_count * channels)
    field = (("rows", 0), ("cols", 1))
    iterate = probe_init.astype(jnp.bfloat16)
    padded_probe = extended(iterate, field, 2, True)

    def power_step(carry, _):
        padded_probe, iterate = carry
        image = conv(padded_probe[None], kernel, False).astype(jnp.bfloat16)
        back = conv(image, kernel, True)[0]
        row_padded = extended(back, field[:1], 2, True)
        squared = butterfly_sum(jnp.sum(back * back), ("rows",))
        squared, row_padded = lax.optimization_barrier((squared, row_padded))
        padded_back = extended(row_padded, field[1:], 2, True)
        squared = butterfly_sum(squared, ("cols",))
        scale_now = jnp.sqrt(squared / count + 1e-06)
        iterate = (back / scale_now).astype(jnp.bfloat16)
        padded_probe = (padded_back / scale_now).astype(jnp.bfloat16)
        return (padded_probe, iterate), scale_now

    padded_both = extended(
        jnp.concatenate([inputs, upstream], axis=0), (("rows", 1), ("cols", 2)), 1, False
    )
    padded_in = padded_both[:batch]
    padded_up = padded_both[batch:]
    outputs = conv(padded_in, kernel, False).astype(jnp.bfloat16)
    input_grad = conv(padded_up, kernel, True).astype(jnp.bfloat16)
    local_grad = lax.conv_general_dilated(
        padded_in,
        upstream,
        window_strides=(1, 1),
        padding="VALID",
        dimension_numbers=("CHWN", "IHWO", "CHWN"),
        preferred_element_type=jnp.float32,
    ).reshape(channels, 9 * channels)
    local_grad, outputs, input_grad, padded_probe = lax.optimization_barrier(
        (local_grad, outputs, input_grad, padded_probe)
    )
    (padded_probe, iterate), norm_trace = lax.scan(
        power_step, (padded_probe, iterate), None, length=ITERS - 1
    )
    image = conv(padded_probe[None], kernel, False).astype(jnp.bfloat16)
    back = conv(image, kernel, True)[0]
    wide_iter = iterate.astype(jnp.float32)
    totals = butterfly_sum(
        jnp.stack([jnp.sum(back * back), jnp.sum(wide_iter * wide_iter)]),
        ("rows", "cols"),
    )
    sum_back = totals[0]
    sum_probe = totals[1]
    lipschitz = jnp.sqrt(jnp.sqrt(sum_back / sum_probe))
    probe_out = back / jnp.sqrt(sum_back / count + 1e-06)
    owned = halving_scatter(local_grad, ("rows", "cols"))
    owned = butterfly_sum(owned, ("rep",))
    total_cells = batch * lax.axis_size("rep") * height * rows_count * breadth * cols_count
    kernel_grad = owned * (1.0 / math.sqrt(total_cells))
    return (outputs, input_grad, kernel_grad, probe_out, lipschitz, norm_trace)


def solution(mesh):
    placed = (
        P("rep", "rows", "cols", None),
        P("rep", "rows", "cols", None),
        P(),
        P("rows", "cols", None),
    )
    return jax.shard_map(
        per_device,
        mesh=mesh,
        in_specs=placed,
        out_specs=(
            P("rep", "rows", "cols", None),
            P("rep", "rows", "cols", None),
            P(("rows", "cols"), None),
            P("rows", "cols", None),
            P(),
            P(),
        ),
        check_vma=False,
    )
```

```python
import math

import jax
import jax.numpy as jnp
from jax import lax
from jax.sharding import PartitionSpec as P

ITERS = 4


def extended(cells, sides, width, closed):
    for axis, dim in sides:
        count = lax.axis_size(axis)
        ends = count if closed else count - 1
        head = lax.slice_in_dim(cells, 0, width, axis=dim)
        tail = lax.slice_in_dim(cells, cells.shape[dim] - width, cells.shape[dim], axis=dim)
        cells = jnp.concatenate(
            [
                lax.ppermute(tail, axis, [(i, (i + 1) % count) for i in range(ends)]),
                cells,
                lax.ppermute(head, axis, [((i + 1) % count, i) for i in range(ends)]),
            ],
            axis=dim,
        )
    return cells


def butterfly_sum(value, axes):
    for axis in axes:
        count = lax.axis_size(axis)
        step = 1
        while step < count:
            value = value + lax.ppermute(value, axis, [(i, i ^ step) for i in range(count)])
            step *= 2
    return value


def halving_scatter(value, axes):
    for axis in axes:
        count = lax.axis_size(axis)
        index = lax.axis_index(axis)
        step = count // 2
        while step >= 1:
            half = value.shape[0] // 2
            upper = (index // step) % 2
            keep = lax.dynamic_slice_in_dim(value, upper * half, half, axis=0)
            send = lax.dynamic_slice_in_dim(value, (1 - upper) * half, half, axis=0)
            if send.size * 8 > 256 * 2304:
                send = send.astype(jnp.bfloat16)
            received = lax.ppermute(send, axis, [(i, i ^ step) for i in range(count)])
            value = keep + received.astype(jnp.float32)
            step //= 2
    return value


def conv(padded, weights, adjoint):
    if adjoint:
        weights = weights[::-1, ::-1]
    return lax.conv_general_dilated(
        padded,
        weights,
        window_strides=(1, 1),
        padding="VALID",
        dimension_numbers=("NHWC", "HWOI" if adjoint else "HWIO", "NHWC"),
        preferred_element_type=jnp.float32,
    )


def per_device(inputs, upstream, kernel, probe_init):
    batch = inputs.shape[0]
    height = inputs.shape[1]
    breadth = inputs.shape[2]
    channels = kernel.shape[2]
    rows_count = lax.axis_size("rows")
    cols_count = lax.axis_size("cols")
    count = float(height * rows_count * breadth * cols_count * channels)
    field = (("rows", 0), ("cols", 1))
    iterate = probe_init.astype(jnp.bfloat16)
    padded_probe = extended(iterate, field, 2, True)

    def power_step(carry, _):
        padded_probe, iterate = carry
        image = conv(padded_probe[None], kernel, False).astype(jnp.bfloat16)
        back = conv(image, kernel, True)[0]
        row_padded = extended(back, field[:1], 2, True)
        squared = butterfly_sum(jnp.sum(back * back), ("rows",))
        squared, row_padded = lax.optimization_barrier((squared, row_padded))
        padded_back = extended(row_padded, field[1:], 2, True)
        squared = butterfly_sum(squared, ("cols",))
        scale_now = jnp.sqrt(squared / count + 1e-06)
        iterate = (back / scale_now).astype(jnp.bfloat16)
        padded_probe = (padded_back / scale_now).astype(jnp.bfloat16)
        return (padded_probe, iterate), scale_now

    padded_both = extended(
        jnp.concatenate([inputs, upstream], axis=0), (("rows", 1), ("cols", 2)), 1, False
    )
    padded_in = padded_both[:batch]
    padded_up = padded_both[batch:]
    outputs = conv(padded_in, kernel, False).astype(jnp.bfloat16)
    input_grad = conv(padded_up, kernel, True).astype(jnp.bfloat16)
    local_grad = lax.conv_general_dilated(
        padded_in,
        upstream,
        window_strides=(1, 1),
        padding="VALID",
        dimension_numbers=("CHWN", "IHWO", "CHWN"),
        preferred_element_type=jnp.float32,
    ).reshape(channels, 9 * channels)
    local_grad, outputs, input_grad, padded_probe = lax.optimization_barrier(
        (local_grad, outputs, input_grad, padded_probe)
    )
    (padded_probe, iterate), norm_trace = lax.scan(
        power_step, (padded_probe, iterate), None, length=ITERS - 1
    )
    image = conv(padded_probe[None], kernel, False).astype(jnp.bfloat16)
    back = conv(image, kernel, True)[0]
    wide_iter = iterate.astype(jnp.float32)
    totals = butterfly_sum(
        jnp.stack([jnp.sum(back * back), jnp.sum(wide_iter * wide_iter)]),
        ("rows", "cols"),
    )
    sum_back = totals[0]
    sum_probe = totals[1]
    lipschitz = jnp.sqrt(jnp.sqrt(sum_back / sum_probe))
    probe_out = back / jnp.sqrt(sum_back / count + 1e-06)
    owned = halving_scatter(local_grad, ("rows", "cols"))
    owned = butterfly_sum(owned, ("rep",))
    total_cells = batch * lax.axis_size("rep") * height * rows_count * breadth * cols_count
    kernel_grad = owned * (1.0 / math.sqrt(total_cells))
    return (outputs, input_grad, kernel_grad, probe_out, lipschitz, norm_trace)


def solution(mesh):
    placed = (
        P("rep", "rows", "cols", None),
        P("rep", "rows", "cols", None),
        P(),
        P("rows", "cols", None),
    )
    return jax.shard_map(
        per_device,
        mesh=mesh,
        in_specs=placed,
        out_specs=(
            P("rep", "rows", "cols", None),
            P("rep", "rows", "cols", None),
            P(("rows", "cols"), None),
            P("rows", "cols", None),
            P(),
            P(),
        ),
        check_vma=False,
    )
```

```python
import math

import jax
import jax.numpy as jnp
from jax import lax
from jax.sharding import PartitionSpec as P

ITERS = 4


def extended(cells, sides, width, closed):
    for axis, dim in sides:
        count = lax.axis_size(axis)
        ends = count if closed else count - 1
        head = lax.slice_in_dim(cells, 0, width, axis=dim)
        tail = lax.slice_in_dim(cells, cells.shape[dim] - width, cells.shape[dim], axis=dim)
        cells = jnp.concatenate(
            [
                lax.ppermute(tail, axis, [(i, (i + 1) % count) for i in range(ends)]),
                cells,
                lax.ppermute(head, axis, [((i + 1) % count, i) for i in range(ends)]),
            ],
            axis=dim,
        )
    return cells


def butterfly_sum(value, axes):
    for axis in axes:
        count = lax.axis_size(axis)
        step = 1
        while step < count:
            value = value + lax.ppermute(value, axis, [(i, i ^ step) for i in range(count)])
            step *= 2
    return value


def halving_scatter(value, axes):
    for axis in axes:
        count = lax.axis_size(axis)
        index = lax.axis_index(axis)
        step = count // 2
        while step >= 1:
            half = value.shape[0] // 2
            upper = (index // step) % 2
            keep = lax.dynamic_slice_in_dim(value, upper * half, half, axis=0)
            send = lax.dynamic_slice_in_dim(value, (1 - upper) * half, half, axis=0)
            if send.size * 32 > 256 * 2304:
                send = send.astype(jnp.bfloat16)
            received = lax.ppermute(send, axis, [(i, i ^ step) for i in range(count)])
            value = keep + received.astype(jnp.float32)
            step //= 2
    return value


def conv(padded, weights, adjoint):
    if adjoint:
        weights = weights[::-1, ::-1]
    return lax.conv_general_dilated(
        padded,
        weights,
        window_strides=(1, 1),
        padding="VALID",
        dimension_numbers=("NHWC", "HWOI" if adjoint else "HWIO", "NHWC"),
        preferred_element_type=jnp.float32,
    )


def per_device(inputs, upstream, kernel, probe_init):
    batch = inputs.shape[0]
    height = inputs.shape[1]
    breadth = inputs.shape[2]
    channels = kernel.shape[2]
    rows_count = lax.axis_size("rows")
    cols_count = lax.axis_size("cols")
    count = float(height * rows_count * breadth * cols_count * channels)
    field = (("rows", 0), ("cols", 1))
    iterate = probe_init.astype(jnp.bfloat16)
    padded_probe = extended(iterate, field, 2, True)

    def power_step(carry, _):
        padded_probe, iterate = carry
        image = conv(padded_probe[None], kernel, False).astype(jnp.bfloat16)
        back = conv(image, kernel, True)[0]
        row_padded = extended(back, field[:1], 2, True)
        squared = butterfly_sum(jnp.sum(back * back), ("rows",))
        squared, row_padded = lax.optimization_barrier((squared, row_padded))
        padded_back = extended(row_padded, field[1:], 2, True)
        squared = butterfly_sum(squared, ("cols",))
        scale_now = jnp.sqrt(squared / count + 1e-06)
        iterate = (back / scale_now).astype(jnp.bfloat16)
        padded_probe = (padded_back / scale_now).astype(jnp.bfloat16)
        return (padded_probe, iterate), scale_now

    padded_both = extended(
        jnp.concatenate([inputs, upstream], axis=0), (("rows", 1), ("cols", 2)), 1, False
    )
    padded_in = padded_both[:batch]
    padded_up = padded_both[batch:]
    outputs = conv(padded_in, kernel, False).astype(jnp.bfloat16)
    input_grad = conv(padded_up, kernel, True).astype(jnp.bfloat16)
    local_grad = lax.conv_general_dilated(
        padded_in,
        upstream,
        window_strides=(1, 1),
        padding="VALID",
        dimension_numbers=("CHWN", "IHWO", "CHWN"),
        preferred_element_type=jnp.float32,
    ).reshape(channels, 9 * channels)
    local_grad, outputs, input_grad, padded_probe = lax.optimization_barrier(
        (local_grad, outputs, input_grad, padded_probe)
    )
    (padded_probe, iterate), norm_trace = lax.scan(
        power_step, (padded_probe, iterate), None, length=ITERS - 1
    )
    image = conv(padded_probe[None], kernel, False).astype(jnp.bfloat16)
    back = conv(image, kernel, True)[0]
    wide_iter = iterate.astype(jnp.float32)
    totals = butterfly_sum(
        jnp.stack([jnp.sum(back * back), jnp.sum(wide_iter * wide_iter)]),
        ("rows", "cols"),
    )
    sum_back = totals[0]
    sum_probe = totals[1]
    lipschitz = jnp.sqrt(jnp.sqrt(sum_back / sum_probe))
    probe_out = back / jnp.sqrt(sum_back / count + 1e-06)
    owned = halving_scatter(local_grad, ("rows", "cols"))
    owned = butterfly_sum(owned, ("rep",))
    total_cells = batch * lax.axis_size("rep") * height * rows_count * breadth * cols_count
    kernel_grad = owned * (1.0 / math.sqrt(total_cells))
    return (outputs, input_grad, kernel_grad, probe_out, lipschitz, norm_trace)


def solution(mesh):
    placed = (
        P("rep", "rows", "cols", None),
        P("rep", "rows", "cols", None),
        P(),
        P("rows", "cols", None),
    )
    return jax.shard_map(
        per_device,
        mesh=mesh,
        in_specs=placed,
        out_specs=(
            P("rep", "rows", "cols", None),
            P("rep", "rows", "cols", None),
            P(("rows", "cols"), None),
            P("rows", "cols", None),
            P(),
            P(),
        ),
        check_vma=False,
    )
```

```python
import math

import jax
import jax.numpy as jnp
from jax import lax
from jax.sharding import PartitionSpec as P

ITERS = 4


def extended(cells, sides, width, closed):
    for axis, dim in sides:
        count = lax.axis_size(axis)
        ends = count if closed else count - 1
        head = lax.slice_in_dim(cells, 0, width, axis=dim)
        tail = lax.slice_in_dim(cells, cells.shape[dim] - width, cells.shape[dim], axis=dim)
        cells = jnp.concatenate(
            [
                lax.ppermute(tail, axis, [(i, (i + 1) % count) for i in range(ends)]),
                cells,
                lax.ppermute(head, axis, [((i + 1) % count, i) for i in range(ends)]),
            ],
            axis=dim,
        )
    return cells


def butterfly_sum(value, axes):
    for axis in axes:
        count = lax.axis_size(axis)
        step = 1
        while step < count:
            value = value + lax.ppermute(value, axis, [(i, i ^ step) for i in range(count)])
            step *= 2
    return value


def extended_pair(field, cells, sides, field_width):
    for axis, field_dim, cells_dim in sides:
        count = lax.axis_size(axis)
        index = lax.axis_index(axis)
        parts = []
        for start, width, dim, array in (
            (0, field_width, field_dim, field),
            (0, 1, cells_dim, cells),
        ):
            parts.append(
                (
                    lax.slice_in_dim(array, 0, width, axis=dim),
                    lax.slice_in_dim(array, array.shape[dim] - width, array.shape[dim], axis=dim),
                )
            )
        channels = field.shape[-1]

        def travel(pieces, pairs):
            flat = jnp.concatenate([piece.reshape(-1, channels) for piece in pieces], axis=0)
            moved = lax.ppermute(flat, axis, pairs)
            split = pieces[0].size // channels
            return (
                moved[:split].reshape(pieces[0].shape),
                moved[split:].reshape(pieces[1].shape),
            )

        field_top, cells_top = travel(
            (parts[0][1], parts[1][1]), [(i, (i + 1) % count) for i in range(count)]
        )
        field_bottom, cells_bottom = travel(
            (parts[0][0], parts[1][0]), [((i + 1) % count, i) for i in range(count)]
        )
        cells_top = jnp.where(index == 0, jnp.zeros_like(cells_top), cells_top)
        cells_bottom = jnp.where(index == count - 1, jnp.zeros_like(cells_bottom), cells_bottom)
        field = jnp.concatenate([field_top, field, field_bottom], axis=field_dim)
        cells = jnp.concatenate([cells_top, cells, cells_bottom], axis=cells_dim)
    return field, cells


def halving_scatter(value, axes):
    for axis in axes:
        count = lax.axis_size(axis)
        index = lax.axis_index(axis)
        step = count // 2
        while step >= 1:
            half = value.shape[0] // 2
            upper = (index // step) % 2
            keep = lax.dynamic_slice_in_dim(value, upper * half, half, axis=0)
            send = lax.dynamic_slice_in_dim(value, (1 - upper) * half, half, axis=0)
            if send.size * 32 > 256 * 2304:
                send = send.astype(jnp.bfloat16)
            received = lax.ppermute(send, axis, [(i, i ^ step) for i in range(count)])
            value = keep + received.astype(jnp.float32)
            step //= 2
    return value


def conv(padded, weights, adjoint):
    if adjoint:
        weights = weights[::-1, ::-1]
    return lax.conv_general_dilated(
        padded,
        weights,
        window_strides=(1, 1),
        padding="VALID",
        dimension_numbers=("NHWC", "HWOI" if adjoint else "HWIO", "NHWC"),
        preferred_element_type=jnp.float32,
    )


def per_device(inputs, upstream, kernel, probe_init):
    batch = inputs.shape[0]
    height = inputs.shape[1]
    breadth = inputs.shape[2]
    channels = kernel.shape[2]
    rows_count = lax.axis_size("rows")
    cols_count = lax.axis_size("cols")
    count = float(height * rows_count * breadth * cols_count * channels)
    field = (("rows", 0), ("cols", 1))
    iterate = probe_init.astype(jnp.bfloat16)

    def power_step(carry, _):
        padded_probe, iterate = carry
        image = conv(padded_probe[None], kernel, False).astype(jnp.bfloat16)
        back = conv(image, kernel, True)[0]
        row_padded = extended(back, field[:1], 2, True)
        squared = butterfly_sum(jnp.sum(back * back), ("rows",))
        squared, row_padded = lax.optimization_barrier((squared, row_padded))
        padded_back = extended(row_padded, field[1:], 2, True)
        squared = butterfly_sum(squared, ("cols",))
        scale_now = jnp.sqrt(squared / count + 1e-06)
        iterate = (back / scale_now).astype(jnp.bfloat16)
        padded_probe = (padded_back / scale_now).astype(jnp.bfloat16)
        return (padded_probe, iterate), scale_now

    padded_probe, padded_both = extended_pair(
        iterate,
        jnp.concatenate([inputs, upstream], axis=0),
        (("rows", 0, 1), ("cols", 1, 2)),
        2,
    )
    padded_in = padded_both[:batch]
    padded_up = padded_both[batch:]
    outputs = conv(padded_in, kernel, False).astype(jnp.bfloat16)
    input_grad = conv(padded_up, kernel, True).astype(jnp.bfloat16)
    local_grad = lax.conv_general_dilated(
        padded_in,
        upstream,
        window_strides=(1, 1),
        padding="VALID",
        dimension_numbers=("CHWN", "IHWO", "CHWN"),
        preferred_element_type=jnp.float32,
    ).reshape(channels, 9 * channels)
    local_grad, outputs, input_grad, padded_probe = lax.optimization_barrier(
        (local_grad, outputs, input_grad, padded_probe)
    )
    (padded_probe, iterate), norm_trace = lax.scan(
        power_step, (padded_probe, iterate), None, length=ITERS - 1
    )
    image = conv(padded_probe[None], kernel, False).astype(jnp.bfloat16)
    back = conv(image, kernel, True)[0]
    wide_iter = iterate.astype(jnp.float32)
    totals = butterfly_sum(
        jnp.stack([jnp.sum(back * back), jnp.sum(wide_iter * wide_iter)]),
        ("rows", "cols"),
    )
    sum_back = totals[0]
    sum_probe = totals[1]
    lipschitz = jnp.sqrt(jnp.sqrt(sum_back / sum_probe))
    probe_out = back / jnp.sqrt(sum_back / count + 1e-06)
    owned = halving_scatter(local_grad, ("rows", "cols"))
    owned = butterfly_sum(owned, ("rep",))
    total_cells = batch * lax.axis_size("rep") * height * rows_count * breadth * cols_count
    kernel_grad = owned * (1.0 / math.sqrt(total_cells))
    return (outputs, input_grad, kernel_grad, probe_out, lipschitz, norm_trace)


def solution(mesh):
    placed = (
        P("rep", "rows", "cols", None),
        P("rep", "rows", "cols", None),
        P(),
        P("rows", "cols", None),
    )
    return jax.shard_map(
        per_device,
        mesh=mesh,
        in_specs=placed,
        out_specs=(
            P("rep", "rows", "cols", None),
            P("rep", "rows", "cols", None),
            P(("rows", "cols"), None),
            P("rows", "cols", None),
            P(),
            P(),
        ),
        check_vma=False,
    )
```

```python
import math

import jax
import jax.numpy as jnp
from jax import lax
from jax.sharding import PartitionSpec as P

ITERS = 4


def extended(cells, sides, width, closed):
    for axis, dim in sides:
        count = lax.axis_size(axis)
        ends = count if closed else count - 1
        head = lax.slice_in_dim(cells, 0, width, axis=dim)
        tail = lax.slice_in_dim(cells, cells.shape[dim] - width, cells.shape[dim], axis=dim)
        cells = jnp.concatenate(
            [
                lax.ppermute(tail, axis, [(i, (i + 1) % count) for i in range(ends)]),
                cells,
                lax.ppermute(head, axis, [((i + 1) % count, i) for i in range(ends)]),
            ],
            axis=dim,
        )
    return cells


def butterfly_sum(value, axes):
    for axis in axes:
        count = lax.axis_size(axis)
        step = 1
        while step < count:
            value = value + lax.ppermute(value, axis, [(i, i ^ step) for i in range(count)])
            step *= 2
    return value


def extended_pair(field, cells, sides, field_width):
    for axis, field_dim, cells_dim in sides:
        count = lax.axis_size(axis)
        index = lax.axis_index(axis)
        parts = []
        for start, width, dim, array in (
            (0, field_width, field_dim, field),
            (0, 1, cells_dim, cells),
        ):
            parts.append(
                (
                    lax.slice_in_dim(array, 0, width, axis=dim),
                    lax.slice_in_dim(array, array.shape[dim] - width, array.shape[dim], axis=dim),
                )
            )
        channels = field.shape[-1]

        def travel(pieces, pairs):
            flat = jnp.concatenate([piece.reshape(-1, channels) for piece in pieces], axis=0)
            moved = lax.ppermute(flat, axis, pairs)
            split = pieces[0].size // channels
            return (
                moved[:split].reshape(pieces[0].shape),
                moved[split:].reshape(pieces[1].shape),
            )

        field_top, cells_top = travel(
            (parts[0][1], parts[1][1]), [(i, (i + 1) % count) for i in range(count)]
        )
        field_bottom, cells_bottom = travel(
            (parts[0][0], parts[1][0]), [((i + 1) % count, i) for i in range(count)]
        )
        cells_top = jnp.where(index == 0, jnp.zeros_like(cells_top), cells_top)
        cells_bottom = jnp.where(index == count - 1, jnp.zeros_like(cells_bottom), cells_bottom)
        field = jnp.concatenate([field_top, field, field_bottom], axis=field_dim)
        cells = jnp.concatenate([cells_top, cells, cells_bottom], axis=cells_dim)
    return field, cells


def halving_scatter(value, axes):
    for axis in axes:
        count = lax.axis_size(axis)
        index = lax.axis_index(axis)
        step = count // 2
        while step >= 1:
            half = value.shape[0] // 2
            upper = (index // step) % 2
            keep = lax.dynamic_slice_in_dim(value, upper * half, half, axis=0)
            send = lax.dynamic_slice_in_dim(value, (1 - upper) * half, half, axis=0)
            send = send.astype(jnp.bfloat16)
            received = lax.ppermute(send, axis, [(i, i ^ step) for i in range(count)])
            value = keep + received.astype(jnp.float32)
            step //= 2
    return value


def conv(padded, weights, adjoint):
    if adjoint:
        weights = weights[::-1, ::-1]
    return lax.conv_general_dilated(
        padded,
        weights,
        window_strides=(1, 1),
        padding="VALID",
        dimension_numbers=("NHWC", "HWOI" if adjoint else "HWIO", "NHWC"),
        preferred_element_type=jnp.float32,
    )


def per_device(inputs, upstream, kernel, probe_init):
    batch = inputs.shape[0]
    height = inputs.shape[1]
    breadth = inputs.shape[2]
    channels = kernel.shape[2]
    rows_count = lax.axis_size("rows")
    cols_count = lax.axis_size("cols")
    count = float(height * rows_count * breadth * cols_count * channels)
    field = (("rows", 0), ("cols", 1))
    iterate = probe_init.astype(jnp.bfloat16)

    def power_step(carry, _):
        padded_probe, iterate = carry
        image = conv(padded_probe[None], kernel, False).astype(jnp.bfloat16)
        back = conv(image, kernel, True)[0]
        row_padded = extended(back, field[:1], 2, True)
        squared = butterfly_sum(jnp.sum(back * back), ("rows",))
        squared, row_padded = lax.optimization_barrier((squared, row_padded))
        padded_back = extended(row_padded, field[1:], 2, True)
        squared = butterfly_sum(squared, ("cols",))
        scale_now = jnp.sqrt(squared / count + 1e-06)
        iterate = (back / scale_now).astype(jnp.bfloat16)
        padded_probe = (padded_back / scale_now).astype(jnp.bfloat16)
        return (padded_probe, iterate), scale_now

    padded_probe, padded_both = extended_pair(
        iterate,
        jnp.concatenate([inputs, upstream], axis=0),
        (("rows", 0, 1), ("cols", 1, 2)),
        2,
    )
    padded_in = padded_both[:batch]
    padded_up = padded_both[batch:]
    outputs = conv(padded_in, kernel, False).astype(jnp.bfloat16)
    input_grad = conv(padded_up, kernel, True).astype(jnp.bfloat16)
    local_grad = lax.conv_general_dilated(
        padded_in,
        upstream,
        window_strides=(1, 1),
        padding="VALID",
        dimension_numbers=("CHWN", "IHWO", "CHWN"),
        preferred_element_type=jnp.float32,
    ).reshape(channels, 9 * channels)
    local_grad, outputs, input_grad, padded_probe = lax.optimization_barrier(
        (local_grad, outputs, input_grad, padded_probe)
    )
    (padded_probe, iterate), norm_trace = lax.scan(
        power_step, (padded_probe, iterate), None, length=ITERS - 1
    )
    image = conv(padded_probe[None], kernel, False).astype(jnp.bfloat16)
    back = conv(image, kernel, True)[0]
    wide_iter = iterate.astype(jnp.float32)
    totals = butterfly_sum(
        jnp.stack([jnp.sum(back * back), jnp.sum(wide_iter * wide_iter)]),
        ("rows", "cols"),
    )
    sum_back = totals[0]
    sum_probe = totals[1]
    lipschitz = jnp.sqrt(jnp.sqrt(sum_back / sum_probe))
    probe_out = back / jnp.sqrt(sum_back / count + 1e-06)
    owned = halving_scatter(local_grad, ("rows", "cols"))
    owned = butterfly_sum(owned, ("rep",))
    total_cells = batch * lax.axis_size("rep") * height * rows_count * breadth * cols_count
    kernel_grad = owned * (1.0 / math.sqrt(total_cells))
    return (outputs, input_grad, kernel_grad, probe_out, lipschitz, norm_trace)


def solution(mesh):
    placed = (
        P("rep", "rows", "cols", None),
        P("rep", "rows", "cols", None),
        P(),
        P("rows", "cols", None),
    )
    return jax.shard_map(
        per_device,
        mesh=mesh,
        in_specs=placed,
        out_specs=(
            P("rep", "rows", "cols", None),
            P("rep", "rows", "cols", None),
            P(("rows", "cols"), None),
            P("rows", "cols", None),
            P(),
            P(),
        ),
        check_vma=False,
    )
```

```python
import math

import jax
import jax.numpy as jnp
from jax import lax
from jax.sharding import PartitionSpec as P

ITERS = 4


def extended(cells, sides, width, closed):
    for axis, dim in sides:
        count = lax.axis_size(axis)
        ends = count if closed else count - 1
        head = lax.slice_in_dim(cells, 0, width, axis=dim)
        tail = lax.slice_in_dim(cells, cells.shape[dim] - width, cells.shape[dim], axis=dim)
        cells = jnp.concatenate(
            [
                lax.ppermute(tail, axis, [(i, (i + 1) % count) for i in range(ends)]),
                cells,
                lax.ppermute(head, axis, [((i + 1) % count, i) for i in range(ends)]),
            ],
            axis=dim,
        )
    return cells


def butterfly_sum(value, axes):
    for axis in axes:
        count = lax.axis_size(axis)
        step = 1
        while step < count:
            value = value + lax.ppermute(value, axis, [(i, i ^ step) for i in range(count)])
            step *= 2
    return value


def extended_pair(field, cells, sides, field_width):
    for axis, field_dim, cells_dim in sides:
        count = lax.axis_size(axis)
        index = lax.axis_index(axis)
        parts = []
        for start, width, dim, array in (
            (0, field_width, field_dim, field),
            (0, 1, cells_dim, cells),
        ):
            parts.append(
                (
                    lax.slice_in_dim(array, 0, width, axis=dim),
                    lax.slice_in_dim(array, array.shape[dim] - width, array.shape[dim], axis=dim),
                )
            )
        channels = field.shape[-1]

        def travel(pieces, pairs):
            flat = jnp.concatenate([piece.reshape(-1, channels) for piece in pieces], axis=0)
            moved = lax.ppermute(flat, axis, pairs)
            split = pieces[0].size // channels
            return (
                moved[:split].reshape(pieces[0].shape),
                moved[split:].reshape(pieces[1].shape),
            )

        field_top, cells_top = travel(
            (parts[0][1], parts[1][1]), [(i, (i + 1) % count) for i in range(count)]
        )
        field_bottom, cells_bottom = travel(
            (parts[0][0], parts[1][0]), [((i + 1) % count, i) for i in range(count)]
        )
        cells_top = jnp.where(index == 0, jnp.zeros_like(cells_top), cells_top)
        cells_bottom = jnp.where(index == count - 1, jnp.zeros_like(cells_bottom), cells_bottom)
        field = jnp.concatenate([field_top, field, field_bottom], axis=field_dim)
        cells = jnp.concatenate([cells_top, cells, cells_bottom], axis=cells_dim)
    return field, cells


def halving_scatter(value, axes):
    for axis in axes:
        count = lax.axis_size(axis)
        index = lax.axis_index(axis)
        step = count // 2
        while step >= 1:
            half = value.shape[0] // 2
            upper = (index // step) % 2
            keep = lax.dynamic_slice_in_dim(value, upper * half, half, axis=0)
            send = lax.dynamic_slice_in_dim(value, (1 - upper) * half, half, axis=0)
            if send.size * 32 > 256 * 2304:
                send = send.astype(jnp.bfloat16)
            received = lax.ppermute(send, axis, [(i, i ^ step) for i in range(count)])
            value = keep + received.astype(jnp.float32)
            step //= 2
    return value


def conv(padded, weights, adjoint):
    if adjoint:
        weights = weights[::-1, ::-1]
    return lax.conv_general_dilated(
        padded,
        weights,
        window_strides=(1, 1),
        padding="VALID",
        dimension_numbers=("NHWC", "HWOI" if adjoint else "HWIO", "NHWC"),
        preferred_element_type=jnp.float32,
    )


def per_device(inputs, upstream, kernel, probe_init):
    batch = inputs.shape[0]
    height = inputs.shape[1]
    breadth = inputs.shape[2]
    channels = kernel.shape[2]
    rows_count = lax.axis_size("rows")
    cols_count = lax.axis_size("cols")
    count = float(height * rows_count * breadth * cols_count * channels)
    field = (("rows", 0), ("cols", 1))
    iterate = probe_init.astype(jnp.bfloat16)

    def power_step(carry, _):
        padded_probe, iterate = carry
        image = conv(padded_probe[None], kernel, False).astype(jnp.bfloat16)
        back = conv(image, kernel, True)[0]
        row_padded = extended(back, field[:1], 2, True)
        squared = butterfly_sum(jnp.sum(back * back), ("rows",))
        squared, row_padded = lax.optimization_barrier((squared, row_padded))
        padded_back = extended(row_padded, field[1:], 2, True)
        squared = butterfly_sum(squared, ("cols",))
        scale_now = jnp.sqrt(squared / count + 1e-06)
        padded_probe = (padded_back / scale_now).astype(jnp.bfloat16)
        return (padded_probe, iterate), scale_now

    padded_probe, padded_both = extended_pair(
        iterate,
        jnp.concatenate([inputs, upstream], axis=0),
        (("rows", 0, 1), ("cols", 1, 2)),
        2,
    )
    padded_in = padded_both[:batch]
    padded_up = padded_both[batch:]
    outputs = conv(padded_in, kernel, False).astype(jnp.bfloat16)
    input_grad = conv(padded_up, kernel, True).astype(jnp.bfloat16)
    local_grad = lax.conv_general_dilated(
        padded_in,
        upstream,
        window_strides=(1, 1),
        padding="VALID",
        dimension_numbers=("CHWN", "IHWO", "CHWN"),
        preferred_element_type=jnp.float32,
    ).reshape(channels, 9 * channels)
    local_grad, outputs, input_grad, padded_probe = lax.optimization_barrier(
        (local_grad, outputs, input_grad, padded_probe)
    )
    (padded_probe, iterate), norm_trace = lax.scan(
        power_step, (padded_probe, iterate), None, length=ITERS - 1
    )
    image = conv(padded_probe[None], kernel, False).astype(jnp.bfloat16)
    back = conv(image, kernel, True)[0]
    wide_iter = padded_probe[2:-2, 2:-2].astype(jnp.float32)
    totals = butterfly_sum(
        jnp.stack([jnp.sum(back * back), jnp.sum(wide_iter * wide_iter)]),
        ("rows", "cols"),
    )
    sum_back = totals[0]
    sum_probe = totals[1]
    lipschitz = jnp.sqrt(jnp.sqrt(sum_back / sum_probe))
    probe_out = back / jnp.sqrt(sum_back / count + 1e-06)
    owned = halving_scatter(local_grad, ("rows", "cols"))
    owned = butterfly_sum(owned, ("rep",))
    total_cells = batch * lax.axis_size("rep") * height * rows_count * breadth * cols_count
    kernel_grad = owned * (1.0 / math.sqrt(total_cells))
    return (outputs, input_grad, kernel_grad, probe_out, lipschitz, norm_trace)


def solution(mesh):
    placed = (
        P("rep", "rows", "cols", None),
        P("rep", "rows", "cols", None),
        P(),
        P("rows", "cols", None),
    )
    return jax.shard_map(
        per_device,
        mesh=mesh,
        in_specs=placed,
        out_specs=(
            P("rep", "rows", "cols", None),
            P("rep", "rows", "cols", None),
            P(("rows", "cols"), None),
            P("rows", "cols", None),
            P(),
            P(),
        ),
        check_vma=False,
    )
```
